128 devices in a mesh: sens: 8 (over z, x_hi), loc: 16 (over y, x_lo, core).
Axes of the slice: x: 4 (x_hi: 2, x_lo: 2; x = x_hi * 2 + x_lo), y: 4, z: 4, core: 2. Of those that a mesh axis runs over, the one named last changes fastest.
Arguments:
- green: bfloat16 [16384, 48, 3, 256], P('loc', 'sens'), may hold values from -0.03125 to 0.03125
- records_buffer: bfloat16 [16, 2, 48, 3, 1024], P('loc', None, 'sens'), may hold values from -6 to 6
- owners: int32 [2], replicated, may hold values from 0 to 15
- onsets: int32 [2, 48], P(None, 'sens'), may hold values from 0 to 257
- codes: int32 [48, 3], P('sens'), may hold values from 0 to 3
Outputs:
- stack: float32 [16384, 2, 512], P(('loc', 'sens'))
The draws below stay inside these ranges and needn't reach their ends.
Inputs may be any that keep to these rules, and one draw needn't show every extreme that they name: `onsets`: a window of 767 samples starting at the offset lies inside the record. `owners`: the block whose buffer holds the event's records. `codes`: a component with code q has weight 2 to the power -q.
All inputs are finite; a program needn't handle non-finite values.
Results may differ from the reference program's by a relative error of at most 0.0003.
Values may be sent and summed in bfloat16 or wider, within the bound.
No kernel may reach another device: no remote copies, remote signals or barrier semaphores. Data moves between devices by JAX's collectives and lax.ppermute only.
A program may use at most 128 MiB of HBM per device.

```python
import jax
import jax.numpy as jnp
from jax import lax

SENSORS = 48
NT = 256
LAGS = 512
SAMPLES = 1024
EV = 2
BLOCKS = 16
LOCS = 16384


def set_ends(drawn, stream_key, least, high):
    longest = drawn.shape.index(max(drawn.shape))
    spots = []
    for shift in (0, 1):
        where = [jax.random.randint(jax.random.fold_in(stream_key, axis), (), 0, length) for axis, length in enumerate(drawn.shape)]
        where[longest] = (where[longest] + shift) % drawn.shape[longest]
        spots.append(tuple(where))
    return drawn.at[spots[0]].set(least).at[spots[1]].set(high)


def shard_levels(key, extent, pieces, smallest, top_value):
    loudness = 1.0
    for dim, parts in pieces:
        steps = jax.random.uniform(jax.random.fold_in(jax.random.fold_in(key, 6), dim), (parts,), jnp.float32, smallest / len(pieces), top_value / len(pieces))
        loudness = loudness * jnp.repeat(jnp.exp(steps), extent[dim] // parts).reshape((-1,) + (1,) * (len(extent) - 1 - dim))
    return loudness


def bell_draw(key, shape, spread, limit, pieces=(), kind=jnp.bfloat16):
    factor_of = shard_levels(key, shape, pieces, -0.22, 0.18) if pieces else 1.0
    array = jax.random.normal(key, shape, jnp.float32) * spread * factor_of
    return jnp.minimum(jnp.maximum(array, -limit), limit).astype(kind)


def setup_inputs(seed: int = 0) -> dict:
    keys = jax.random.split(jax.random.key(seed), 6)
    green = bell_draw(keys[0], (LOCS, SENSORS, 3, NT), (SENSORS * 3 * NT) ** -0.5, 0.03125, ((0, 16), (1, 8)))
    records_buffer = bell_draw(keys[1], (BLOCKS, EV, SENSORS, 3, SAMPLES), 1.0, 6.0, ((0, 16), (2, 8)))
    owners = jax.random.randint(keys[2], (EV,), 0, BLOCKS).astype(jnp.int32)
    onsets = set_ends(jax.random.randint(keys[3], (EV, SENSORS), 0, SAMPLES - NT - LAGS + 2), jax.random.fold_in(keys[3], 1), 0, (SAMPLES - NT - LAGS + 2) - 1).astype(jnp.int32)
    codes = set_ends(jax.random.randint(keys[4], (SENSORS, 3), 0, 4), jax.random.fold_in(keys[4], 1), 0, 3).astype(jnp.int32)
    return {"green": green, "records_buffer": records_buffer, "owners": owners, "onsets": onsets, "codes": codes}


def sensor_windows(traces, offsets, weight_codes, length, lag_count):
    def window_of(record_row, begin_at):
        return lax.dynamic_slice_in_dim(record_row, begin_at.astype(jnp.int32), length, 1)

    windows = jax.vmap(window_of)(traces, offsets)
    weighting = jnp.exp2(-weight_codes.astype(jnp.float32))
    weighted = (windows.astype(jnp.float32) * weighting[:, :, None]).astype(jnp.bfloat16)
    tap_count = length - lag_count + 1
    tiled = jnp.tile(weighted, (1, 1, tap_count))
    padded = jnp.concatenate([tiled, jnp.zeros(weighted.shape[:2] + (tap_count,), jnp.bfloat16)], axis=2)
    shaped = padded.reshape(weighted.shape[0], 3, tap_count, length + 1)[..., :lag_count]
    return shaped.reshape(-1, lag_count)


def reference(green, records_buffer, owners, onsets, codes):
    blocks = []
    for event_idx in range(EV):
        traces = records_buffer[owners[event_idx], event_idx]
        blocks.append(sensor_windows(traces, onsets[event_idx], codes, NT + LAGS - 1, LAGS))
    toeplitz = jnp.stack(blocks, axis=1).reshape(blocks[0].shape[0], -1)
    point_rows = green.shape[0]
    product = jnp.dot(green.reshape(point_rows, -1), toeplitz, preferred_element_type=jnp.float32)
    return product.reshape(point_rows, EV, LAGS)
```

```python
import jax
import jax.numpy as jnp
from jax import lax
from jax.sharding import PartitionSpec as P

NT = 256
LAGS = 512
EV = 2


def from_owners(x, axis, roots):
    size = lax.axis_size(axis)
    me = lax.axis_index(axis)
    bit = 1
    while bit < size:
        got = lax.ppermute(x, axis, [(i, i ^ bit) for i in range(size)])
        keep = ((me // bit) % 2) == ((roots // bit) % 2)
        x = jnp.where(keep.reshape((-1,) + (1,) * (x.ndim - 1)), x, got)
        bit *= 2
    return x


def sensor_windows(traces, offsets, weight_codes, length, lag_count):

    def window_of(record_row, begin_at):
        return lax.dynamic_slice_in_dim(record_row, begin_at, length, 1)

    windows = jax.vmap(window_of)(traces, offsets)
    weighting = jnp.exp2(-weight_codes.astype(jnp.float32))
    weighted = (windows.astype(jnp.float32) * weighting[:, :, None]).astype(jnp.bfloat16)
    tap_count = length - lag_count + 1
    tiled = jnp.tile(weighted, (1, 1, tap_count))
    padded = jnp.concatenate(
        [tiled, jnp.zeros(weighted.shape[:2] + (tap_count,), jnp.bfloat16)], axis=2
    )
    shaped = padded.reshape(weighted.shape[0], 3, tap_count, length + 1)[..., :lag_count]
    return shaped.reshape(-1, lag_count)


def local(green, records_buffer, owners, onsets, codes):
    point_rows = green.shape[0]
    flat_green = green.reshape(point_rows, -1)
    length = NT + LAGS - 1
    traces_all = from_owners(records_buffer[0], "loc", owners)
    blocks = []
    for event_idx in range(EV):
        operand = sensor_windows(traces_all[event_idx], onsets[event_idx], codes, length, LAGS)
        blocks.append(operand)
    toeplitz = jnp.stack(blocks, axis=1).reshape(blocks[0].shape[0], -1)
    product = jnp.dot(flat_green, toeplitz, preferred_element_type=jnp.float32)
    return lax.psum_scatter(
        product.reshape(point_rows, EV, LAGS), "sens", scatter_dimension=0, tiled=True
    )


def solution(mesh):
    return jax.shard_map(
        local,
        mesh=mesh,
        in_specs=(
            P("loc", "sens", None, None),
            P("loc", None, "sens", None, None),
            P(),
            P(None, "sens"),
            P("sens", None),
        ),
        out_specs=P(("loc", "sens"), None, None),
        check_vma=False,
    )
```

```python
import jax
import jax.numpy as jnp
from jax import lax
from jax.experimental import pallas as pl
from jax.experimental.pallas import tpu as pltpu
from jax.sharding import Mesh
from jax.sharding import PartitionSpec as P

NT = 256
LAGS = 512
SAMPLES = 1024
EV = 2


def from_owners(x, axis, roots):
    size = lax.axis_size(axis)
    me = lax.axis_index(axis)
    bit = 1
    while bit < size:
        got = lax.ppermute(x, axis, [(i, i ^ bit) for i in range(size)])
        keep = ((me // bit) % 2) == ((roots // bit) % 2)
        x = jnp.where(keep.reshape((-1,) + (1,) * (x.ndim - 1)), x, got)
        bit *= 2
    return x


def _toeplitz_kernel(shift_ref, weight_ref, rev_ref, out_ref):
    sc = pl.program_id(0)
    rows = weight_ref.shape[0]
    w = weight_ref[sc]
    for e in range(rev_ref.shape[1]):
        row = rev_ref[0, e : e + 1, :]
        row = pltpu.roll(row, shift_ref[e * rows + sc], 1)
        row = (row * w).astype(jnp.bfloat16).astype(jnp.float32)
        wide = jnp.broadcast_to(row, (NT, SAMPLES))
        band = pltpu.roll(wide, 0, 1, stride=1, stride_axis=0)
        out_ref[:, e * LAGS : (e + 1) * LAGS] = band[:, :LAGS].astype(out_ref.dtype)


def toeplitz_reversed(traces, onsets, codes):
    ev, sens = traces.shape[0], traces.shape[1]
    rows = sens * 3
    rev = jnp.flip(traces.astype(jnp.float32), axis=-1).reshape(ev, rows, SAMPLES)
    rev = jnp.transpose(rev, (1, 0, 2))
    shifts = jnp.repeat(onsets.astype(jnp.int32), 3, axis=1)
    shifts = ((shifts - LAGS) % SAMPLES).reshape(-1)
    weights = jnp.exp2(-codes.astype(jnp.float32)).reshape(-1)
    return pl.pallas_call(
        _toeplitz_kernel,
        grid_spec=pltpu.PrefetchScalarGridSpec(
            num_scalar_prefetch=1,
            grid=(rows,),
            in_specs=[
                pl.BlockSpec(memory_space=pltpu.SMEM),
                pl.BlockSpec((1, ev, SAMPLES), lambda i, s: (i, 0, 0)),
            ],
            out_specs=pl.BlockSpec((NT, ev * LAGS), lambda i, s: (i, 0)),
        ),
        out_shape=jax.ShapeDtypeStruct((rows * NT, ev * LAGS), jnp.bfloat16),
        cost_estimate=pl.CostEstimate(
            flops=0, transcendentals=0, bytes_accessed=rows * NT * ev * LAGS * 2
        ),
    )(shifts, weights, rev)


def reduce_over_sens(product):
    return lax.psum_scatter(product, SENS_AXES, scatter_dimension=0, tiled=True)


def local(green, records_buffer, owners, onsets, codes):
    point_rows = green.shape[0]
    flat_green = green.reshape(point_rows, -1)
    traces = from_owners(records_buffer[0], "loc", owners)
    toeplitz = toeplitz_reversed(traces, onsets, codes)
    product = jnp.dot(flat_green, toeplitz, preferred_element_type=jnp.float32)
    totals = reduce_over_sens(product.reshape(point_rows, EV, LAGS))
    return jnp.flip(totals, axis=-1)


SENS_AXES = "sens"


def solution(mesh):
    return jax.shard_map(
        local,
        mesh=mesh,
        in_specs=(
            P("loc", "sens", None, None),
            P("loc", None, "sens", None, None),
            P(),
            P(None, "sens"),
            P("sens", None),
        ),
        out_specs=P(("loc", "sens"), None, None),
        check_vma=False,
    )
```

```python
import jax
import jax.numpy as jnp
from jax import lax
from jax.experimental import pallas as pl
from jax.experimental.pallas import tpu as pltpu
from jax.sharding import Mesh
from jax.sharding import PartitionSpec as P

NT = 256
LAGS = 512
SAMPLES = 1024
EV = 2


def from_owners(x, axis, roots):
    size = lax.axis_size(axis)
    me = lax.axis_index(axis)
    bit = 1
    while bit < size:
        got = lax.ppermute(x, axis, [(i, i ^ bit) for i in range(size)])
        keep = ((me // bit) % 2) == ((roots // bit) % 2)
        x = jnp.where(keep.reshape((-1,) + (1,) * (x.ndim - 1)), x, got)
        bit *= 2
    return x


def _toeplitz_kernel(shift_ref, weight_ref, rev_ref, out_ref):
    sc = pl.program_id(0)
    rows = weight_ref.shape[0]
    w = weight_ref[sc]
    for e in range(rev_ref.shape[1]):
        row = rev_ref[0, e : e + 1, :]
        row = pltpu.roll(row, shift_ref[e * rows + sc], 1)
        row = (row * w).astype(jnp.bfloat16).astype(jnp.float32)
        wide = jnp.broadcast_to(row, (NT, SAMPLES))
        band = pltpu.roll(wide, 0, 1, stride=1, stride_axis=0)
        out_ref[:, e * LAGS : (e + 1) * LAGS] = band[:, :LAGS].astype(out_ref.dtype)


def toeplitz_reversed(traces, onsets, codes):
    ev, sens = traces.shape[0], traces.shape[1]
    rows = sens * 3
    rev = jnp.flip(traces.astype(jnp.float32), axis=-1).reshape(ev, rows, SAMPLES)
    rev = jnp.transpose(rev, (1, 0, 2))
    shifts = jnp.repeat(onsets.astype(jnp.int32), 3, axis=1)
    shifts = ((shifts - LAGS) % SAMPLES).reshape(-1)
    weights = jnp.exp2(-codes.astype(jnp.float32)).reshape(-1)
    return pl.pallas_call(
        _toeplitz_kernel,
        grid_spec=pltpu.PrefetchScalarGridSpec(
            num_scalar_prefetch=1,
            grid=(rows,),
            in_specs=[
                pl.BlockSpec(memory_space=pltpu.SMEM),
                pl.BlockSpec((1, ev, SAMPLES), lambda i, s: (i, 0, 0)),
            ],
            out_specs=pl.BlockSpec((NT, ev * LAGS), lambda i, s: (i, 0)),
        ),
        out_shape=jax.ShapeDtypeStruct((rows * NT, ev * LAGS), jnp.bfloat16),
        cost_estimate=pl.CostEstimate(
            flops=0, transcendentals=0, bytes_accessed=rows * NT * ev * LAGS * 2
        ),
    )(shifts, weights, rev)


def reduce_over_sens(halves):
    size = lax.axis_size("sens")
    me = lax.axis_index("sens")
    zs, xs = size // 2, 2
    z, xh = me // xs, me % xs
    quarter = halves[0].shape[0] // zs

    def ring_perm(step):
        return [(i, ((i // xs + step) % zs) * xs + i % xs) for i in range(size)]

    def chunk(x, c):
        return lax.dynamic_slice_in_dim(x, c * quarter, quarter, 0)

    sums = []
    for half, step in zip(halves, (1, zs - 1)):
        acc = chunk(half, (z + zs - step) % zs)
        for k in range(zs - 1):
            got = lax.ppermute(acc, "sens", ring_perm(step))
            c = (z + 4 * zs - step * (k + 2)) % zs
            acc = got + chunk(half, c)
        sums.append(acc)
    mine = jnp.concatenate(sums, axis=1)
    block = quarter // xs
    theirs = lax.dynamic_slice_in_dim(mine, (1 - xh) * block, block, 0)
    kept = lax.dynamic_slice_in_dim(mine, xh * block, block, 0)
    got = lax.ppermute(theirs, "sens", [(i, i ^ 1) for i in range(size)])
    return kept + got


def local(green, records_buffer, owners, onsets, codes):
    point_rows = green.shape[0]
    flat_green = green.reshape(point_rows, -1)
    traces = from_owners(records_buffer[0], "loc", owners)
    toeplitz = toeplitz_reversed(traces, onsets, codes)
    halves = [
        jnp.dot(flat_green, toeplitz[:, e * LAGS : (e + 1) * LAGS], preferred_element_type=jnp.float32)
        for e in range(EV)
    ]
    totals = reduce_over_sens(halves)
    return jnp.flip(totals.reshape(-1, EV, LAGS), axis=-1)


def solution(mesh):
    return jax.shard_map(
        local,
        mesh=mesh,
        in_specs=(
            P("loc", "sens", None, None),
            P("loc", None, "sens", None, None),
            P(),
            P(None, "sens"),
            P("sens", None),
        ),
        out_specs=P(("loc", "sens"), None, None),
        check_vma=False,
    )
```

```python
import jax
import jax.numpy as jnp
from jax import lax
from jax.experimental import pallas as pl
from jax.experimental.pallas import tpu as pltpu
from jax.sharding import Mesh
from jax.sharding import PartitionSpec as P

NT = 256
LAGS = 512
SAMPLES = 1024
EV = 2


def from_owners(x, axis, roots):
    size = lax.axis_size(axis)
    me = lax.axis_index(axis)
    bit = 1
    while bit < size:
        got = lax.ppermute(x, axis, [(i, i ^ bit) for i in range(size)])
        keep = ((me // bit) % 2) == ((roots // bit) % 2)
        x = jnp.where(keep.reshape((-1,) + (1,) * (x.ndim - 1)), x, got)
        bit *= 2
    return x


def _toeplitz_kernel(shift_ref, weight_ref, rev_ref, out_ref):
    sc = pl.program_id(0)
    rows = weight_ref.shape[0]
    w = weight_ref[sc]
    for e in range(rev_ref.shape[1]):
        row = rev_ref[0, e : e + 1, :]
        row = pltpu.roll(row, shift_ref[e * rows + sc], 1)
        row = (row * w).astype(jnp.bfloat16).astype(jnp.float32)
        wide = jnp.broadcast_to(row, (NT, SAMPLES))
        band = pltpu.roll(wide, 0, 1, stride=1, stride_axis=0)
        out_ref[:, e * LAGS : (e + 1) * LAGS] = band[:, :LAGS].astype(out_ref.dtype)


def toeplitz_reversed(traces, onsets, codes):
    ev, sens = traces.shape[0], traces.shape[1]
    rows = sens * 3
    rev = jnp.flip(traces.astype(jnp.float32), axis=-1).reshape(ev, rows, SAMPLES)
    rev = jnp.transpose(rev, (1, 0, 2))
    shifts = jnp.repeat(onsets.astype(jnp.int32), 3, axis=1)
    shifts = ((shifts - LAGS) % SAMPLES).reshape(-1)
    weights = jnp.exp2(-codes.astype(jnp.float32)).reshape(-1)
    return pl.pallas_call(
        _toeplitz_kernel,
        grid_spec=pltpu.PrefetchScalarGridSpec(
            num_scalar_prefetch=1,
            grid=(rows,),
            in_specs=[
                pl.BlockSpec(memory_space=pltpu.SMEM),
                pl.BlockSpec((1, ev, SAMPLES), lambda i, s: (i, 0, 0)),
            ],
            out_specs=pl.BlockSpec((NT, ev * LAGS), lambda i, s: (i, 0)),
        ),
        out_shape=jax.ShapeDtypeStruct((rows * NT, ev * LAGS), jnp.bfloat16),
        cost_estimate=pl.CostEstimate(
            flops=0, transcendentals=0, bytes_accessed=rows * NT * ev * LAGS * 2
        ),
    )(shifts, weights, rev)


def reduce_over_sens(halves):
    size = lax.axis_size("sens")
    me = lax.axis_index("sens")
    zs, xs = size // 2, 2
    z, xh = me // xs, me % xs
    quarter = halves[0].shape[0] // zs

    def ring_perm(step):
        return [(i, ((i // xs + step) % zs) * xs + i % xs) for i in range(size)]

    def chunk(x, c):
        return lax.dynamic_slice_in_dim(x, c * quarter, quarter, 0)

    sums = []
    for half, step in zip(halves, (1, zs - 1)):
        acc = chunk(half, (z + zs - step) % zs)
        for k in range(zs - 1):
            got = lax.ppermute(acc, "sens", ring_perm(step))
            c = (z + 4 * zs - step * (k + 2)) % zs
            acc = got + chunk(half, c)
        sums.append(acc)
    mine = jnp.concatenate(sums, axis=1)
    block = quarter // xs
    theirs = lax.dynamic_slice_in_dim(mine, (1 - xh) * block, block, 0)
    kept = lax.dynamic_slice_in_dim(mine, xh * block, block, 0)
    got = lax.ppermute(theirs, "sens", [(i, i ^ 1) for i in range(size)])
    return kept + got


def local(green, records_buffer, owners, onsets, codes):
    point_rows = green.shape[0]
    flat_green = green.reshape(point_rows, -1)
    traces = from_owners(records_buffer[0], "loc", owners)
    toeplitz = toeplitz_reversed(traces, onsets, codes)
    rows = green.shape[1] * green.shape[2]
    green_t = jnp.transpose(green, (1, 2, 0, 3)).reshape(rows, point_rows, NT)
    toeplitz = toeplitz.reshape(rows, NT, EV * LAGS)
    halves = [
        jnp.einsum(
            "rpt,rtn->pn",
            green_t,
            toeplitz[:, :, e * LAGS : (e + 1) * LAGS],
            preferred_element_type=jnp.float32,
        )
        for e in range(EV)
    ]
    totals = reduce_over_sens(halves)
    return jnp.flip(totals.reshape(-1, EV, LAGS), axis=-1)


def solution(mesh):
    return jax.shard_map(
        local,
        mesh=mesh,
        in_specs=(
            P("loc", "sens", None, None),
            P("loc", None, "sens", None, None),
            P(),
            P(None, "sens"),
            P("sens", None),
        ),
        out_specs=P(("loc", "sens"), None, None),
        check_vma=False,
    )
```

```python
import jax
import jax.numpy as jnp
from jax import lax
from jax.experimental import pallas as pl
from jax.experimental.pallas import tpu as pltpu
from jax.sharding import PartitionSpec as P

NT = 256
LAGS = 512
SAMPLES = 1024
EV = 2
WIDE = LAGS + NT


def from_owners(x, axis, roots, radix=4):
    size = lax.axis_size(axis)
    me = lax.axis_index(axis)
    span = 1
    while span < size:
        radix = min(radix, size // span)
        digit = (roots // span) % radix
        mine = (me // span) % radix
        out = x
        for d in range(1, radix):
            perm = [(i, i - ((i // span) % radix) * span + (((i // span) % radix + d) % radix) * span) for i in range(size)]
            got = lax.ppermute(x, axis, perm)
            src = (mine + radix - d) % radix
            out = jnp.where((src == digit).reshape((-1,) + (1,) * (x.ndim - 1)), got, out)
        x = out
        span *= radix
    return x


def _toeplitz_kernel(shift_ref, weight_ref, rev_ref, out_ref):
    sc = pl.program_id(0)
    row = rev_ref[0]
    row = pltpu.roll(row, shift_ref[sc], 1)
    row = (row * weight_ref[sc]).astype(jnp.bfloat16).astype(jnp.float32)
    row = jnp.concatenate([row[:, :LAGS], row[:, SAMPLES - NT :]], axis=1)
    wide = jnp.broadcast_to(row, (NT, WIDE))
    band = pltpu.roll(wide, 0, 1, stride=1, stride_axis=0)
    out_ref[...] = band[:, :LAGS].astype(out_ref.dtype)


def toeplitz_reversed(rev, shifts, weights):
    rows = rev.shape[0]
    return pl.pallas_call(
        _toeplitz_kernel,
        grid_spec=pltpu.PrefetchScalarGridSpec(
            num_scalar_prefetch=1,
            grid=(rows,),
            in_specs=[
                pl.BlockSpec(memory_space=pltpu.SMEM),
                pl.BlockSpec((1, 1, SAMPLES), lambda i, s: (i, 0, 0)),
            ],
            out_specs=pl.BlockSpec((NT, LAGS), lambda i, s: (i, 0)),
        ),
        out_shape=jax.ShapeDtypeStruct((rows * NT, LAGS), jnp.bfloat16),
        cost_estimate=pl.CostEstimate(flops=0, transcendentals=0, bytes_accessed=rows * NT * LAGS * 2),
    )(shifts, weights, rev)


def local(green, records_buffer, owners, onsets, codes):
    point_rows = green.shape[0]
    rows = green.shape[1] * green.shape[2]
    green_t = jnp.transpose(green, (1, 2, 0, 3)).reshape(rows, point_rows, NT)
    flipped = jnp.flip(records_buffer[0], axis=-1)
    traces = from_owners(flipped, "loc", owners)
    rev = traces.astype(jnp.float32).reshape(EV, rows, 1, SAMPLES)
    shifts = (jnp.repeat(onsets.astype(jnp.int32), 3, axis=1) - LAGS) % SAMPLES
    weights = jnp.exp2(-codes.astype(jnp.float32)).reshape(-1)

    size = lax.axis_size("sens")
    me = lax.axis_index("sens")
    xs = 2
    zs = size // xs
    z, xh = me // xs, me % xs
    quarter = point_rows // zs
    block = quarter // xs

    def piece(band, c):
        g = lax.dynamic_slice_in_dim(green_t, c * quarter, quarter, 1)
        return jnp.einsum("rpt,rtn->pn", g, band.reshape(rows, NT, LAGS), preferred_element_type=jnp.float32)

    def ring_perm(step):
        return [(i, ((i // xs + step) % zs) * xs + i % xs) for i in range(size)]

    outs = []
    for e, step in zip(range(EV), (1, zs - 1)):
        band = toeplitz_reversed(rev[e], shifts[e], weights)
        acc = piece(band, (z + zs - step) % zs)
        for k in range(zs - 1):
            got = lax.ppermute(acc, "sens", ring_perm(step))
            acc = got + piece(band, (z + 4 * zs - step * (k + 2)) % zs)
        theirs = lax.dynamic_slice_in_dim(acc, (1 - xh) * block, block, 0)
        kept = lax.dynamic_slice_in_dim(acc, xh * block, block, 0)
        got = lax.ppermute(theirs, "sens", [(i, i ^ 1) for i in range(size)])
        outs.append(jnp.flip(kept, axis=-1) + jnp.flip(got, axis=-1))
    return jnp.stack(outs, axis=1)


def solution(mesh):
    return jax.shard_map(
        local,
        mesh=mesh,
        in_specs=(
            P("loc", "sens", None, None),
            P("loc", None, "sens", None, None),
            P(),
            P(None, "sens"),
            P("sens", None),
        ),
        out_specs=P(("loc", "sens"), None, None),
        check_vma=False,
    )
```

```python
import jax
import jax.numpy as jnp
from jax import lax
from jax.experimental import pallas as pl
from jax.experimental.pallas import tpu as pltpu
from jax.sharding import PartitionSpec as P

NT = 256
LAGS = 512
SAMPLES = 1024
EV = 2
WIDE = LAGS + NT


def from_owners(x, axis, roots, radix=4):
    size = lax.axis_size(axis)
    me = lax.axis_index(axis)
    span = 1
    while span < size:
        radix = min(radix, size // span)
        digit = (roots // span) % radix
        mine = (me // span) % radix
        out = x
        for d in range(1, radix):
            perm = [(i, i - ((i // span) % radix) * span + (((i // span) % radix + d) % radix) * span) for i in range(size)]
            got = lax.ppermute(x, axis, perm)
            src = (mine + radix - d) % radix
            out = jnp.where((src == digit).reshape((-1,) + (1,) * (x.ndim - 1)), got, out)
        x = out
        span *= radix
    return x


def _toeplitz_kernel(shift_ref, weight_ref, rev_ref, out_ref):
    def body(r, carry):
        row = rev_ref[r]
        row = pltpu.roll(row, shift_ref[r], 1)
        row = (row * weight_ref[r]).astype(jnp.bfloat16).astype(jnp.float32)
        row = jnp.concatenate([row[:, :LAGS], row[:, SAMPLES - NT :]], axis=1)
        wide = jnp.broadcast_to(row, (NT, WIDE))
        band = pltpu.roll(wide, 0, 1, stride=1, stride_axis=0)
        out_ref[pl.ds(pl.multiple_of(r * NT, NT), NT), :] = band[:, :LAGS].astype(out_ref.dtype)
        return carry

    lax.fori_loop(0, rev_ref.shape[0], body, 0)


def toeplitz_reversed(rev, shifts, weights):
    rows = rev.shape[0]
    return pl.pallas_call(
        _toeplitz_kernel,
        in_specs=[
            pl.BlockSpec(memory_space=pltpu.SMEM),
            pl.BlockSpec(memory_space=pltpu.SMEM),
            pl.BlockSpec(memory_space=pltpu.VMEM),
        ],
        out_specs=pl.BlockSpec(memory_space=pltpu.VMEM),
        out_shape=jax.ShapeDtypeStruct((rows * NT, LAGS), jnp.bfloat16),
        cost_estimate=pl.CostEstimate(flops=0, transcendentals=0, bytes_accessed=rows * NT * LAGS * 2),
    )(shifts, weights, rev)


def local(green, records_buffer, owners, onsets, codes):
    point_rows = green.shape[0]
    rows = green.shape[1] * green.shape[2]
    green_t = jnp.transpose(green, (1, 2, 0, 3)).reshape(rows, point_rows, NT)
    flipped = jnp.flip(records_buffer[0], axis=-1)
    traces = from_owners(flipped, "loc", owners)
    rev = traces.astype(jnp.float32).reshape(EV, rows, 1, SAMPLES)
    shifts = (jnp.repeat(onsets.astype(jnp.int32), 3, axis=1) - LAGS) % SAMPLES
    weights = jnp.exp2(-codes.astype(jnp.float32)).reshape(-1)

    size = lax.axis_size("sens")
    me = lax.axis_index("sens")
    xs = 2
    zs = size // xs
    z, xh = me // xs, me % xs
    quarter = point_rows // zs
    block = quarter // xs

    def piece(band, c):
        g = lax.dynamic_slice_in_dim(green_t, c * quarter, quarter, 1)
        return jnp.einsum("rpt,rtn->pn", g, band.reshape(rows, NT, LAGS), preferred_element_type=jnp.float32)

    def ring_perm(step):
        return [(i, ((i // xs + step) % zs) * xs + i % xs) for i in range(size)]

    outs = []
    for e, step in zip(range(EV), (1, zs - 1)):
        band = toeplitz_reversed(rev[e], shifts[e], weights)
        acc = piece(band, (z + zs - step) % zs)
        for k in range(zs - 1):
            got = lax.ppermute(acc, "sens", ring_perm(step))
            acc = got + piece(band, (z + 4 * zs - step * (k + 2)) % zs)
        theirs = lax.dynamic_slice_in_dim(acc, (1 - xh) * block, block, 0)
        kept = lax.dynamic_slice_in_dim(acc, xh * block, block, 0)
        got = lax.ppermute(theirs, "sens", [(i, i ^ 1) for i in range(size)])
        outs.append(jnp.flip(kept, axis=-1) + jnp.flip(got, axis=-1))
    return jnp.stack(outs, axis=1)


def solution(mesh):
    return jax.shard_map(
        local,
        mesh=mesh,
        in_specs=(
            P("loc", "sens", None, None),
            P("loc", None, "sens", None, None),
            P(),
            P(None, "sens"),
            P("sens", None),
        ),
        out_specs=P(("loc", "sens"), None, None),
        check_vma=False,
    )
```

```python
import jax
import jax.numpy as jnp
from jax import lax
from jax.experimental import pallas as pl
from jax.experimental.pallas import tpu as pltpu
from jax.sharding import PartitionSpec as P

NT = 256
LAGS = 512
SAMPLES = 1024
EV = 2
WIDE = LAGS + NT


def from_owners(x, axis, roots, radix=16):
    size = lax.axis_size(axis)
    me = lax.axis_index(axis)
    span = 1
    while span < size:
        radix = min(radix, size // span)
        digit = (roots // span) % radix
        mine = (me // span) % radix
        out = x
        for d in range(1, radix):
            perm = [(i, i - ((i // span) % radix) * span + (((i // span) % radix + d) % radix) * span) for i in range(size)]
            got = lax.ppermute(x, axis, perm)
            src = (mine + radix - d) % radix
            out = jnp.where((src == digit).reshape((-1,) + (1,) * (x.ndim - 1)), got, out)
        x = out
        span *= radix
    return x


def _toeplitz_kernel(shift_ref, weight_ref, rev_ref, out_ref):
    def body(r, carry):
        row = rev_ref[r]
        row = pltpu.roll(row, shift_ref[r], 1)
        row = (row * weight_ref[r]).astype(jnp.bfloat16).astype(jnp.float32)
        row = jnp.concatenate([row[:, :LAGS], row[:, SAMPLES - NT :]], axis=1)
        wide = jnp.broadcast_to(row, (NT, WIDE))
        band = pltpu.roll(wide, 0, 1, stride=1, stride_axis=0)
        out_ref[pl.ds(pl.multiple_of(r * NT, NT), NT), :] = band[:, :LAGS].astype(out_ref.dtype)
        return carry

    lax.fori_loop(0, rev_ref.shape[0], body, 0)


def toeplitz_reversed(rev, shifts, weights):
    rows = rev.shape[0]
    return pl.pallas_call(
        _toeplitz_kernel,
        in_specs=[
            pl.BlockSpec(memory_space=pltpu.SMEM),
            pl.BlockSpec(memory_space=pltpu.SMEM),
            pl.BlockSpec(memory_space=pltpu.VMEM),
        ],
        out_specs=pl.BlockSpec(memory_space=pltpu.VMEM),
        out_shape=jax.ShapeDtypeStruct((rows * NT, LAGS), jnp.bfloat16),
        cost_estimate=pl.CostEstimate(flops=0, transcendentals=0, bytes_accessed=rows * NT * LAGS * 2),
    )(shifts, weights, rev)


def local(green, records_buffer, owners, onsets, codes):
    point_rows = green.shape[0]
    rows = green.shape[1] * green.shape[2]
    green_t = jnp.transpose(green, (1, 2, 0, 3)).reshape(rows, point_rows, NT)
    flipped = jnp.flip(records_buffer[0], axis=-1)
    traces = from_owners(flipped, "loc", owners)
    rev = traces.astype(jnp.float32).reshape(EV * rows, 1, SAMPLES)
    shifts = ((jnp.repeat(onsets.astype(jnp.int32), 3, axis=1) - LAGS) % SAMPLES).reshape(-1)
    weights = jnp.tile(jnp.exp2(-codes.astype(jnp.float32)).reshape(-1), EV)
    bands = toeplitz_reversed(rev, shifts, weights).reshape(EV, rows * NT, LAGS)

    size = lax.axis_size("sens")
    me = lax.axis_index("sens")
    xs = 2
    zs = size // xs
    z, xh = me // xs, me % xs
    quarter = point_rows // zs
    block = quarter // xs

    def piece(band, c):
        g = lax.dynamic_slice_in_dim(green_t, c * quarter, quarter, 1)
        return jnp.einsum("rpt,rtn->pn", g, band.reshape(rows, NT, LAGS), preferred_element_type=jnp.float32)

    def ring_perm(step):
        return [(i, ((i // xs + step) % zs) * xs + i % xs) for i in range(size)]

    outs = []
    for e, step in zip(range(EV), (1, zs - 1)):
        band = bands[e]
        acc = piece(band, (z + zs - step) % zs)
        for k in range(zs - 1):
            got = lax.ppermute(acc, "sens", ring_perm(step))
            acc = got + piece(band, (z + 4 * zs - step * (k + 2)) % zs)
        theirs = lax.dynamic_slice_in_dim(acc, (1 - xh) * block, block, 0)
        kept = lax.dynamic_slice_in_dim(acc, xh * block, block, 0)
        got = lax.ppermute(theirs, "sens", [(i, i ^ 1) for i in range(size)])
        outs.append(jnp.flip(kept, axis=-1) + jnp.flip(got, axis=-1))
    return jnp.stack(outs, axis=1)


def solution(mesh):
    return jax.shard_map(
        local,
        mesh=mesh,
        in_specs=(
            P("loc", "sens", None, None),
            P("loc", None, "sens", None, None),
            P(),
            P(None, "sens"),
            P("sens", None),
        ),
        out_specs=P(("loc", "sens"), None, None),
        check_vma=False,
    )
```

```python
import jax
import jax.numpy as jnp
from jax import lax
from jax.experimental import pallas as pl
from jax.experimental.pallas import tpu as pltpu
from jax.sharding import PartitionSpec as P

NT = 256
LAGS = 512
SAMPLES = 1024
EV = 2
WIDE = LAGS + NT


def from_owners(x, axis, roots, radix=4):
    size = lax.axis_size(axis)
    me = lax.axis_index(axis)
    span = 1
    while span < size:
        radix = min(radix, size // span)
        digit = (roots // span) % radix
        mine = (me // span) % radix
        out = x
        for d in range(1, radix):
            perm = [(i, i - ((i // span) % radix) * span + (((i // span) % radix + d) % radix) * span) for i in range(size)]
            got = lax.ppermute(x, axis, perm)
            src = (mine + radix - d) % radix
            out = jnp.where((src == digit).reshape((-1,) + (1,) * (x.ndim - 1)), got, out)
        x = out
        span *= radix
    return x


def _toeplitz_kernel(shift_ref, weight_ref, rev_ref, *out_refs):
    rows = weight_ref.shape[0]

    def body(r, carry):
        for e, out_ref in enumerate(out_refs):
            row = rev_ref[e * rows + r]
            row = pltpu.roll(row, shift_ref[e * rows + r], 1)
            row = (row * weight_ref[r]).astype(jnp.bfloat16).astype(jnp.float32)
            row = jnp.concatenate([row[:, :LAGS], row[:, SAMPLES - NT :]], axis=1)
            wide = jnp.broadcast_to(row, (NT, WIDE))
            band = pltpu.roll(wide, 0, 1, stride=1, stride_axis=0)
            out_ref[pl.ds(pl.multiple_of(r * NT, NT), NT), :] = band[:, :LAGS].astype(out_ref.dtype)
        return carry

    lax.fori_loop(0, rows, body, 0)


def toeplitz_reversed(rev, shifts, weights):
    rows = weights.shape[0]
    ev = rev.shape[0] // rows
    band = jax.ShapeDtypeStruct((rows * NT, LAGS), jnp.bfloat16)
    return pl.pallas_call(
        _toeplitz_kernel,
        in_specs=[
            pl.BlockSpec(memory_space=pltpu.SMEM),
            pl.BlockSpec(memory_space=pltpu.SMEM),
            pl.BlockSpec(memory_space=pltpu.VMEM),
        ],
        out_specs=[pl.BlockSpec(memory_space=pltpu.VMEM)] * ev,
        out_shape=[band] * ev,
        cost_estimate=pl.CostEstimate(flops=0, transcendentals=0, bytes_accessed=ev * rows * NT * LAGS * 2),
    )(shifts, weights, rev)


def local(green, records_buffer, owners, onsets, codes):
    point_rows = green.shape[0]
    rows = green.shape[1] * green.shape[2]
    green_t = jnp.transpose(green, (1, 2, 0, 3)).reshape(rows, point_rows, NT)
    flipped = jnp.flip(records_buffer[0], axis=-1)
    traces = from_owners(flipped, "loc", owners)
    rev = traces.astype(jnp.float32).reshape(EV * rows, 1, SAMPLES)
    shifts = ((jnp.repeat(onsets.astype(jnp.int32), 3, axis=1) - LAGS) % SAMPLES).reshape(-1)
    weights = jnp.exp2(-codes.astype(jnp.float32)).reshape(-1)
    bands = toeplitz_reversed(rev, shifts, weights)

    size = lax.axis_size("sens")
    me = lax.axis_index("sens")
    xs = 2
    zs = size // xs
    z, xh = me // xs, me % xs
    quarter = point_rows // zs
    block = quarter // xs

    def piece(band, c):
        g = lax.dynamic_slice_in_dim(green_t, c * quarter, quarter, 1)
        return jnp.einsum("rpt,rtn->pn", g, band.reshape(rows, NT, LAGS), preferred_element_type=jnp.float32)

    def ring_perm(step):
        return [(i, ((i // xs + step) % zs) * xs + i % xs) for i in range(size)]

    outs = []
    for e, step in zip(range(EV), (1, zs - 1)):
        band = bands[e]
        acc = piece(band, (z + zs - step) % zs)
        for k in range(zs - 1):
            got = lax.ppermute(acc, "sens", ring_perm(step))
            acc = got + piece(band, (z + 4 * zs - step * (k + 2)) % zs)
        theirs = lax.dynamic_slice_in_dim(acc, (1 - xh) * block, block, 0)
        kept = lax.dynamic_slice_in_dim(acc, xh * block, block, 0)
        got = lax.ppermute(theirs, "sens", [(i, i ^ 1) for i in range(size)])
        outs.append(jnp.flip(kept, axis=-1) + jnp.flip(got, axis=-1))
    return jnp.stack(outs, axis=1)


def solution(mesh):
    return jax.shard_map(
        local,
        mesh=mesh,
        in_specs=(
            P("loc", "sens", None, None),
            P("loc", None, "sens", None, None),
            P(),
            P(None, "sens"),
            P("sens", None),
        ),
        out_specs=P(("loc", "sens"), None, None),
        check_vma=False,
    )
```

```python
import jax
import jax.numpy as jnp
from jax import lax
from jax.experimental import pallas as pl
from jax.experimental.pallas import tpu as pltpu
from jax.sharding import PartitionSpec as P

NT = 256
LAGS = 512
SAMPLES = 1024
EV = 2
WIDE = LAGS + NT


def from_owners(x, axis, roots, radix=4):
    size = lax.axis_size(axis)
    me = lax.axis_index(axis)
    span = 1
    while span < size:
        radix = min(radix, size // span)
        digit = (roots // span) % radix
        mine = (me // span) % radix
        out = x
        for d in range(1, radix):
            perm = [(i, i - ((i // span) % radix) * span + (((i // span) % radix + d) % radix) * span) for i in range(size)]
            got = lax.ppermute(x, axis, perm)
            src = (mine + radix - d) % radix
            out = jnp.where((src == digit).reshape((-1,) + (1,) * (x.ndim - 1)), got, out)
        x = out
        span *= radix
    return x


def _toeplitz_kernel(shift_ref, weight_ref, rev_ref, *out_refs):
    rows = weight_ref.shape[0]

    def body(r, carry):
        for e, out_ref in enumerate(out_refs):
            row = rev_ref[e * rows + r]
            row = pltpu.roll(row, shift_ref[e * rows + r], 1)
            row = (row * weight_ref[r]).astype(jnp.bfloat16).astype(jnp.float32)
            row = jnp.concatenate([row[:, :LAGS], row[:, SAMPLES - NT :]], axis=1)
            wide = jnp.broadcast_to(row, (NT, WIDE))
            band = pltpu.roll(wide, 0, 1, stride=1, stride_axis=0)
            out_ref[pl.ds(pl.multiple_of(r * NT, NT), NT), :] = band[:, :LAGS].astype(out_ref.dtype)
        return carry

    lax.fori_loop(0, rows, body, 0)


def toeplitz_reversed(rev, shifts, weights):
    rows = weights.shape[0]
    ev = rev.shape[0] // rows
    band = jax.ShapeDtypeStruct((rows * NT, LAGS), jnp.bfloat16)
    return pl.pallas_call(
        _toeplitz_kernel,
        in_specs=[
            pl.BlockSpec(memory_space=pltpu.SMEM),
            pl.BlockSpec(memory_space=pltpu.SMEM),
            pl.BlockSpec(memory_space=pltpu.VMEM),
        ],
        out_specs=[pl.BlockSpec(memory_space=pltpu.VMEM)] * ev,
        out_shape=[band] * ev,
        cost_estimate=pl.CostEstimate(flops=0, transcendentals=0, bytes_accessed=ev * rows * NT * LAGS * 2),
    )(shifts, weights, rev)


def local(green, records_buffer, owners, onsets, codes):
    point_rows = green.shape[0]
    rows = green.shape[1] * green.shape[2]
    green_t = jnp.transpose(green, (1, 2, 0, 3)).reshape(rows, point_rows, NT)
    flipped = jnp.flip(records_buffer[0], axis=-1)
    traces = from_owners(flipped, "loc", owners)
    rev = traces.astype(jnp.float32).reshape(EV * rows, 1, SAMPLES)
    shifts = ((jnp.repeat(onsets.astype(jnp.int32), 3, axis=1) - LAGS) % SAMPLES).reshape(-1)
    weights = jnp.exp2(-codes.astype(jnp.float32)).reshape(-1)
    bands = toeplitz_reversed(rev, shifts, weights)

    size = lax.axis_size("sens")
    me = lax.axis_index("sens")
    xs = 2
    zs = size // xs
    z, xh = me // xs, me % xs
    quarter = point_rows // zs
    block = quarter // xs

    def piece(band, c):
        g = lax.dynamic_slice_in_dim(green_t, c * quarter, quarter, 1)
        return jnp.einsum("rpt,rtn->pn", g, band.reshape(rows, NT, LAGS), preferred_element_type=jnp.float32)

    def ring_perm(step):
        return [(i, ((i // xs + step) % zs) * xs + i % xs) for i in range(size)]

    outs = []
    for e, step in zip(range(EV), (1, zs - 1)):
        band = bands[e]
        acc = piece(band, (z + zs - step) % zs)
        for k in range(zs - 1):
            got = lax.ppermute(acc, "sens", ring_perm(step))
            part = lax.optimization_barrier(piece(band, (z + 4 * zs - step * (k + 2)) % zs))
            acc = got + part
        theirs = lax.dynamic_slice_in_dim(acc, (1 - xh) * block, block, 0)
        kept = lax.dynamic_slice_in_dim(acc, xh * block, block, 0)
        got = lax.ppermute(theirs, "sens", [(i, i ^ 1) for i in range(size)])
        outs.append(jnp.flip(kept, axis=-1) + jnp.flip(got, axis=-1))
    return jnp.stack(outs, axis=1)


def solution(mesh):
    return jax.shard_map(
        local,
        mesh=mesh,
        in_specs=(
            P("loc", "sens", None, None),
            P("loc", None, "sens", None, None),
            P(),
            P(None, "sens"),
            P("sens", None),
        ),
        out_specs=P(("loc", "sens"), None, None),
        check_vma=False,
    )
```

```python
import jax
import jax.numpy as jnp
from jax import lax
from jax.experimental import pallas as pl
from jax.experimental.pallas import tpu as pltpu
from jax.sharding import PartitionSpec as P

NT = 256
LAGS = 512
SAMPLES = 1024
EV = 2
WIDE = LAGS + NT
HALF = LAGS // 2


def from_owners(x, axis, roots, radix=4):
    size = lax.axis_size(axis)
    me = lax.axis_index(axis)
    span = 1
    while span < size:
        radix = min(radix, size // span)
        digit = (roots // span) % radix
        mine = (me // span) % radix
        out = x
        for d in range(1, radix):
            perm = [(i, i - ((i // span) % radix) * span + (((i // span) % radix + d) % radix) * span) for i in range(size)]
            got = lax.ppermute(x, axis, perm)
            src = (mine + radix - d) % radix
            out = jnp.where((src == digit).reshape((-1,) + (1,) * (x.ndim - 1)), got, out)
        x = out
        span *= radix
    return x


def _toeplitz_kernel(shift_ref, weight_ref, rev_ref, *out_refs):
    rows = weight_ref.shape[0]

    def body(r, carry):
        for e in range(len(out_refs) // 2):
            out_ref = out_refs[2 * e : 2 * e + 2]
            row = rev_ref[e * rows + r]
            row = pltpu.roll(row, shift_ref[e * rows + r], 1)
            row = (row * weight_ref[r]).astype(jnp.bfloat16).astype(jnp.float32)
            row = jnp.concatenate([row[:, :LAGS], row[:, SAMPLES - NT :]], axis=1)
            wide = jnp.broadcast_to(row, (NT, WIDE))
            band = pltpu.roll(wide, 0, 1, stride=1, stride_axis=0)
            at = pl.ds(pl.multiple_of(r * NT, NT), NT)
            for h, ref in enumerate(out_ref):
                ref[at, :] = band[:, h * HALF : (h + 1) * HALF].astype(ref.dtype)
        return carry

    lax.fori_loop(0, rows, body, 0)


def toeplitz_reversed(rev, shifts, weights):
    rows = weights.shape[0]
    ev = rev.shape[0] // rows
    band = jax.ShapeDtypeStruct((rows * NT, HALF), jnp.bfloat16)
    return pl.pallas_call(
        _toeplitz_kernel,
        in_specs=[
            pl.BlockSpec(memory_space=pltpu.SMEM),
            pl.BlockSpec(memory_space=pltpu.SMEM),
            pl.BlockSpec(memory_space=pltpu.VMEM),
        ],
        out_specs=[pl.BlockSpec(memory_space=pltpu.VMEM)] * (2 * ev),
        out_shape=[band] * (2 * ev),
        cost_estimate=pl.CostEstimate(flops=0, transcendentals=0, bytes_accessed=ev * rows * NT * LAGS * 2),
    )(shifts, weights, rev)


def local(green, records_buffer, owners, onsets, codes):
    point_rows = green.shape[0]
    rows = green.shape[1] * green.shape[2]
    green_t = jnp.transpose(green, (1, 2, 0, 3)).reshape(rows, point_rows, NT)
    flipped = jnp.flip(records_buffer[0], axis=-1)
    traces = from_owners(flipped, "loc", owners)
    rev = traces.astype(jnp.float32).reshape(EV * rows, 1, SAMPLES)
    shifts = ((jnp.repeat(onsets.astype(jnp.int32), 3, axis=1) - LAGS) % SAMPLES).reshape(-1)
    weights = jnp.exp2(-codes.astype(jnp.float32)).reshape(-1)
    bands = toeplitz_reversed(rev, shifts, weights)

    size = lax.axis_size("sens")
    me = lax.axis_index("sens")
    xs = 2
    zs = size // xs
    z, xh = me // xs, me % xs
    quarter = point_rows // zs
    block = quarter // xs

    def piece(band, start, count):
        g = lax.dynamic_slice_in_dim(green_t, start, count, 1)
        return jnp.einsum("rpt,rtn->pn", g, band.reshape(rows, NT, -1), preferred_element_type=jnp.float32)

    def ring_perm(step):
        return [(i, ((i // xs + step) % zs) * xs + i % xs) for i in range(size)]

    swap = [(i, i ^ 1) for i in range(size)]

    outs = []
    for e, step in zip(range(EV), (1, zs - 1)):
        first, second = bands[2 * e], bands[2 * e + 1]

        whole = piece(second, 0, point_rows).reshape(zs, xs, block, HALF)
        theirs = lax.dynamic_index_in_dim(whole, 1 - xh, 1, keepdims=False)
        mine = lax.dynamic_index_in_dim(whole, xh, 1, keepdims=False)
        paired = mine + lax.ppermute(theirs, "sens", swap)
        acc_x = lax.dynamic_index_in_dim(paired, (z + zs - step) % zs, 0, keepdims=False)

        acc_z = piece(first, ((z + zs - step) % zs) * quarter, quarter)
        for k in range(zs - 1):
            c = (z + 4 * zs - step * (k + 2)) % zs
            got_z = lax.ppermute(acc_z, "sens", ring_perm(step))
            part = lax.optimization_barrier(piece(first, c * quarter, quarter))
            acc_z = got_z + part
            got_x = lax.ppermute(acc_x, "sens", ring_perm(step))
            acc_x = got_x + lax.dynamic_index_in_dim(paired, c, 0, keepdims=False)
        theirs = lax.dynamic_slice_in_dim(acc_z, (1 - xh) * block, block, 0)
        kept = lax.dynamic_slice_in_dim(acc_z, xh * block, block, 0)
        acc_z = kept + lax.ppermute(theirs, "sens", swap)
        outs.append(jnp.flip(jnp.concatenate([acc_z, acc_x], axis=1), axis=-1))
    return jnp.stack(outs, axis=1)


def solution(mesh):
    return jax.shard_map(
        local,
        mesh=mesh,
        in_specs=(
            P("loc", "sens", None, None),
            P("loc", None, "sens", None, None),
            P(),
            P(None, "sens"),
            P("sens", None),
        ),
        out_specs=P(("loc", "sens"), None, None),
        check_vma=False,
    )
```

```python
import jax
import jax.numpy as jnp
from jax import lax
from jax.experimental import pallas as pl
from jax.experimental.pallas import tpu as pltpu
from jax.sharding import PartitionSpec as P

NT = 256
LAGS = 512
SAMPLES = 1024
EV = 2
WIDE = LAGS + NT


def from_owners(x, axis, roots, radix=4):
    size = lax.axis_size(axis)
    me = lax.axis_index(axis)
    span = 1
    while span < size:
        radix = min(radix, size // span)
        digit = (roots // span) % radix
        mine = (me // span) % radix
        out = x
        for d in range(1, radix):
            perm = [(i, i - ((i // span) % radix) * span + (((i // span) % radix + d) % radix) * span) for i in range(size)]
            got = lax.ppermute(x, axis, perm)
            src = (mine + radix - d) % radix
            out = jnp.where((src == digit).reshape((-1,) + (1,) * (x.ndim - 1)), got, out)
        x = out
        span *= radix
    return x


def _toeplitz_kernel(shift_ref, weight_ref, rev_ref, *out_refs):
    rows = weight_ref.shape[0]

    def body(r, carry):
        for e, out_ref in enumerate(out_refs):
            row = rev_ref[e * rows + r]
            row = pltpu.roll(row, shift_ref[e * rows + r], 1)
            row = (row * weight_ref[r]).astype(jnp.bfloat16).astype(jnp.float32)
            row = jnp.concatenate([row[:, :LAGS], row[:, SAMPLES - NT :]], axis=1)
            wide = jnp.broadcast_to(row, (NT, WIDE))
            band = pltpu.roll(wide, 0, 1, stride=1, stride_axis=0)
            out_ref[pl.ds(pl.multiple_of(r * NT, NT), NT), :] = band[:, :LAGS].astype(out_ref.dtype)
        return carry

    lax.fori_loop(0, rows, body, 0)


def toeplitz_reversed(rev, shifts, weights):
    rows = weights.shape[0]
    ev = rev.shape[0] // rows
    band = jax.ShapeDtypeStruct((rows * NT, LAGS), jnp.bfloat16)
    return pl.pallas_call(
        _toeplitz_kernel,
        in_specs=[
            pl.BlockSpec(memory_space=pltpu.SMEM),
            pl.BlockSpec(memory_space=pltpu.SMEM),
            pl.BlockSpec(memory_space=pltpu.VMEM),
        ],
        out_specs=[pl.BlockSpec(memory_space=pltpu.VMEM)] * ev,
        out_shape=[band] * ev,
        cost_estimate=pl.CostEstimate(flops=0, transcendentals=0, bytes_accessed=ev * rows * NT * LAGS * 2),
    )(shifts, weights, rev)


def local(green, records_buffer, owners, onsets, codes):
    point_rows = green.shape[0]
    rows = green.shape[1] * green.shape[2]
    green_t = jnp.transpose(green, (1, 2, 0, 3)).reshape(rows, point_rows, NT)
    traces = from_owners(records_buffer[0], "loc", owners).reshape(EV * rows, SAMPLES)
    i = lax.broadcasted_iota(jnp.int32, (SAMPLES, SAMPLES), 0)
    j = lax.broadcasted_iota(jnp.int32, (SAMPLES, SAMPLES), 1)
    anti = (i + j == SAMPLES - 1).astype(jnp.bfloat16)
    rev = jnp.dot(traces, anti, preferred_element_type=jnp.float32).reshape(EV * rows, 1, SAMPLES)
    shifts = ((jnp.repeat(onsets.astype(jnp.int32), 3, axis=1) - LAGS) % SAMPLES).reshape(-1)
    weights = jnp.exp2(-codes.astype(jnp.float32)).reshape(-1)
    bands = toeplitz_reversed(rev, shifts, weights)

    size = lax.axis_size("sens")
    me = lax.axis_index("sens")
    xs = 2
    zs = size // xs
    z, xh = me // xs, me % xs
    quarter = point_rows // zs
    block = quarter // xs

    def piece(band, c):
        g = lax.dynamic_slice_in_dim(green_t, c * quarter, quarter, 1)
        return jnp.einsum("rpt,rtn->pn", g, band.reshape(rows, NT, LAGS), preferred_element_type=jnp.float32)

    def ring_perm(step):
        return [(i, ((i // xs + step) % zs) * xs + i % xs) for i in range(size)]

    steps = (1, zs - 1)
    firsts = lax.optimization_barrier(tuple(piece(bands[e], (z + zs - st) % zs) for e, st in enumerate(steps)))
    outs = []
    for e, step in zip(range(EV), steps):
        band = bands[e]
        acc = firsts[e]
        for k in range(zs - 1):
            got = lax.ppermute(acc, "sens", ring_perm(step))
            part = lax.optimization_barrier(piece(band, (z + 4 * zs - step * (k + 2)) % zs))
            acc = got + part
        theirs = lax.dynamic_slice_in_dim(acc, (1 - xh) * block, block, 0)
        kept = lax.dynamic_slice_in_dim(acc, xh * block, block, 0)
        got = lax.ppermute(theirs, "sens", [(i, i ^ 1) for i in range(size)])
        outs.append(jnp.flip(kept, axis=-1) + jnp.flip(got, axis=-1))
    return jnp.stack(outs, axis=1)


def solution(mesh):
    return jax.shard_map(
        local,
        mesh=mesh,
        in_specs=(
            P("loc", "sens", None, None),
            P("loc", None, "sens", None, None),
            P(),
            P(None, "sens"),
            P("sens", None),
        ),
        out_specs=P(("loc", "sens"), None, None),
        check_vma=False,
    )
```

```python
import jax
import jax.numpy as jnp
from jax import lax
from jax.experimental import pallas as pl
from jax.experimental.pallas import tpu as pltpu
from jax.sharding import PartitionSpec as P

NT = 256
LAGS = 512
SAMPLES = 1024
EV = 2
WIDE = LAGS + NT


def from_owners(x, axis, roots, radix=4):
    size = lax.axis_size(axis)
    me = lax.axis_index(axis)
    span = 1
    while span < size:
        radix = min(radix, size // span)
        digit = (roots // span) % radix
        mine = (me // span) % radix
        out = x
        for d in range(1, radix):
            perm = [(i, i - ((i // span) % radix) * span + (((i // span) % radix + d) % radix) * span) for i in range(size)]
            got = lax.ppermute(x, axis, perm)
            src = (mine + radix - d) % radix
            out = jnp.where((src == digit).reshape((-1,) + (1,) * (x.ndim - 1)), got, out)
        x = out
        span *= radix
    return x


def _toeplitz_kernel(shift_ref, weight_ref, rev_ref, *out_refs):
    rows = weight_ref.shape[0]

    def body(r, carry):
        for e, out_ref in enumerate(out_refs):
            row = rev_ref[e * rows + r]
            row = pltpu.roll(row, shift_ref[e * rows + r], 1)
            row = (row * weight_ref[r]).astype(jnp.bfloat16).astype(jnp.float32)
            row = jnp.concatenate([row[:, :LAGS], row[:, SAMPLES - NT :]], axis=1)
            wide = jnp.broadcast_to(row, (NT, WIDE))
            band = pltpu.roll(wide, 0, 1, stride=1, stride_axis=0)
            out_ref[pl.ds(pl.multiple_of(r * NT, NT), NT), :] = band[:, :LAGS].astype(out_ref.dtype)
        return carry

    lax.fori_loop(0, rows, body, 0)


def toeplitz_reversed(rev, shifts, weights):
    rows = weights.shape[0]
    ev = rev.shape[0] // rows
    band = jax.ShapeDtypeStruct((rows * NT, LAGS), jnp.bfloat16)
    return pl.pallas_call(
        _toeplitz_kernel,
        in_specs=[
            pl.BlockSpec(memory_space=pltpu.SMEM),
            pl.BlockSpec(memory_space=pltpu.SMEM),
            pl.BlockSpec(memory_space=pltpu.VMEM),
        ],
        out_specs=[pl.BlockSpec(memory_space=pltpu.VMEM)] * ev,
        out_shape=[band] * ev,
        cost_estimate=pl.CostEstimate(flops=0, transcendentals=0, bytes_accessed=ev * rows * NT * LAGS * 2),
    )(shifts, weights, rev)


def local(green, records_buffer, owners, onsets, codes):
    point_rows = green.shape[0]
    rows = green.shape[1] * green.shape[2]
    green_t = jnp.transpose(green, (1, 2, 0, 3)).reshape(rows, point_rows, NT)
    traces = from_owners(records_buffer[0], "loc", owners).reshape(EV * rows, SAMPLES)
    i = lax.broadcasted_iota(jnp.int32, (SAMPLES, SAMPLES), 0)
    j = lax.broadcasted_iota(jnp.int32, (SAMPLES, SAMPLES), 1)
    anti = (i + j == SAMPLES - 1).astype(jnp.bfloat16)
    rev = jnp.dot(traces, anti, preferred_element_type=jnp.float32).reshape(EV * rows, 1, SAMPLES)
    shifts = ((jnp.repeat(onsets.astype(jnp.int32), 3, axis=1) - LAGS) % SAMPLES).reshape(-1)
    weights = jnp.exp2(-codes.astype(jnp.float32)).reshape(-1)
    bands = toeplitz_reversed(rev, shifts, weights)

    size = lax.axis_size("sens")
    me = lax.axis_index("sens")
    xs = 2
    zs = size // xs
    z, xh = me // xs, me % xs
    quarter = point_rows // zs
    block = quarter // xs

    def piece(band, c, src=None):
        g = lax.dynamic_slice_in_dim(green_t if src is None else src, c * quarter, quarter, 1)
        return jnp.einsum("rpt,rtn->pn", g, band.reshape(rows, NT, LAGS), preferred_element_type=jnp.float32)

    def ring_perm(step):
        return [(i, ((i // xs + step) % zs) * xs + i % xs) for i in range(size)]

    steps = (1, zs - 1)
    g = green_t

    def ordered(e, c, g):
        return lax.optimization_barrier((piece(bands[e], c, g), green_t))

    accs, gots = [], []
    for e, step in enumerate(steps):
        acc, g = ordered(e, (z + zs - step) % zs, g)
        accs.append(acc)
        gots.append(lax.ppermute(acc, "sens", ring_perm(step)))
    for k in range(zs - 1):
        for e, step in enumerate(steps):
            part, g = ordered(e, (z + 4 * zs - step * (k + 2)) % zs, g)
            accs[e] = gots[e] + part
            if k < zs - 2:
                gots[e] = lax.ppermute(accs[e], "sens", ring_perm(step))
    outs = []
    for e in range(EV):
        theirs = lax.dynamic_slice_in_dim(accs[e], (1 - xh) * block, block, 0)
        kept = lax.dynamic_slice_in_dim(accs[e], xh * block, block, 0)
        got = lax.ppermute(theirs, "sens", [(i, i ^ 1) for i in range(size)])
        outs.append(jnp.flip(kept, axis=-1) + jnp.flip(got, axis=-1))
    return jnp.stack(outs, axis=1)


def solution(mesh):
    return jax.shard_map(
        local,
        mesh=mesh,
        in_specs=(
            P("loc", "sens", None, None),
            P("loc", None, "sens", None, None),
            P(),
            P(None, "sens"),
            P("sens", None),
        ),
        out_specs=P(("loc", "sens"), None, None),
        check_vma=False,
    )
```

```python
import jax
import jax.numpy as jnp
from jax import lax
from jax.experimental import pallas as pl
from jax.experimental.pallas import tpu as pltpu
from jax.sharding import PartitionSpec as P

NT = 256
LAGS = 512
SAMPLES = 1024
EV = 2
WIDE = LAGS + NT
HALF = LAGS // 2


def from_owners(x, axis, roots, radix=4):
    size = lax.axis_size(axis)
    me = lax.axis_index(axis)
    span = 1
    while span < size:
        radix = min(radix, size // span)
        digit = (roots // span) % radix
        mine = (me // span) % radix
        out = x
        for d in range(1, radix):
            perm = [(i, i - ((i // span) % radix) * span + (((i // span) % radix + d) % radix) * span) for i in range(size)]
            got = lax.ppermute(x, axis, perm)
            src = (mine + radix - d) % radix
            out = jnp.where((src == digit).reshape((-1,) + (1,) * (x.ndim - 1)), got, out)
        x = out
        span *= radix
    return x


def _toeplitz_kernel(shift_ref, weight_ref, rev_ref, *out_refs):
    rows = weight_ref.shape[0]

    def body(r, carry):
        for e in range(len(out_refs) // 2):
            out_ref = out_refs[2 * e : 2 * e + 2]
            row = rev_ref[e * rows + r]
            row = pltpu.roll(row, shift_ref[e * rows + r], 1)
            row = (row * weight_ref[r]).astype(jnp.bfloat16).astype(jnp.float32)
            row = jnp.concatenate([row[:, :LAGS], row[:, SAMPLES - NT :]], axis=1)
            wide = jnp.broadcast_to(row, (NT, WIDE))
            band = pltpu.roll(wide, 0, 1, stride=1, stride_axis=0)
            at = pl.ds(pl.multiple_of(r * NT, NT), NT)
            for h, ref in enumerate(out_ref):
                ref[at, :] = band[:, h * HALF : (h + 1) * HALF].astype(ref.dtype)
        return carry

    lax.fori_loop(0, rows, body, 0)


def toeplitz_reversed(rev, shifts, weights):
    rows = weights.shape[0]
    ev = rev.shape[0] // rows
    band = jax.ShapeDtypeStruct((rows * NT, HALF), jnp.bfloat16)
    return pl.pallas_call(
        _toeplitz_kernel,
        in_specs=[
            pl.BlockSpec(memory_space=pltpu.SMEM),
            pl.BlockSpec(memory_space=pltpu.SMEM),
            pl.BlockSpec(memory_space=pltpu.VMEM),
        ],
        out_specs=[pl.BlockSpec(memory_space=pltpu.VMEM)] * (2 * ev),
        out_shape=[band] * (2 * ev),
        cost_estimate=pl.CostEstimate(flops=0, transcendentals=0, bytes_accessed=ev * rows * NT * LAGS * 2),
    )(shifts, weights, rev)


def local(green, records_buffer, owners, onsets, codes):
    point_rows = green.shape[0]
    rows = green.shape[1] * green.shape[2]
    green_t = jnp.transpose(green, (1, 2, 0, 3)).reshape(rows, point_rows, NT)
    traces = from_owners(records_buffer[0], "loc", owners).reshape(EV * rows, SAMPLES)
    i = lax.broadcasted_iota(jnp.int32, (SAMPLES, SAMPLES), 0)
    j = lax.broadcasted_iota(jnp.int32, (SAMPLES, SAMPLES), 1)
    anti = (i + j == SAMPLES - 1).astype(jnp.bfloat16)
    rev = jnp.dot(traces, anti, preferred_element_type=jnp.float32).reshape(EV * rows, 1, SAMPLES)
    shifts = ((jnp.repeat(onsets.astype(jnp.int32), 3, axis=1) - LAGS) % SAMPLES).reshape(-1)
    weights = jnp.exp2(-codes.astype(jnp.float32)).reshape(-1)
    bands = toeplitz_reversed(rev, shifts, weights)

    size = lax.axis_size("sens")
    me = lax.axis_index("sens")
    xs = 2
    zs = size // xs
    z, xh = me // xs, me % xs
    quarter = point_rows // zs
    block = quarter // xs

    def piece(band, start, count, src):
        g = lax.dynamic_slice_in_dim(src, start, count, 1)
        return jnp.einsum("rpt,rtn->pn", g, band.reshape(rows, NT, -1), preferred_element_type=jnp.float32)

    def ordered(band, start, count, g):
        return lax.optimization_barrier((piece(band, start, count, g), green_t))

    def ring_perm(step):
        return [(i, ((i // xs + step) % zs) * xs + i % xs) for i in range(size)]

    swap = [(i, i ^ 1) for i in range(size)]
    steps = (1, zs - 1)

    g = green_t
    acc_z, got_z = [], []
    for e, step in enumerate(steps):
        acc, g = ordered(bands[2 * e], ((z + zs - step) % zs) * quarter, quarter, g)
        acc_z.append(acc)
        got_z.append(lax.ppermute(acc, "sens", ring_perm(step)))
    got_x = []
    for e in range(EV):
        theirs = []
        for q in range(zs):
            part, g = ordered(bands[2 * e + 1], (q * xs + 1 - xh) * block, block, g)
            theirs.append(part)
        got_x.append(lax.ppermute(jnp.stack(theirs), "sens", swap))
    for e, step in enumerate(steps):
        part, g = ordered(bands[2 * e], ((z + 4 * zs - 2 * step) % zs) * quarter, quarter, g)
        acc_z[e] = got_z[e] + part
        got_z[e] = lax.ppermute(acc_z[e], "sens", ring_perm(step))
    paired = []
    for e in range(EV):
        mine = []
        for q in range(zs):
            part, g = ordered(bands[2 * e + 1], (q * xs + xh) * block, block, g)
            mine.append(part)
        paired.append(jnp.stack(mine) + got_x[e])
    acc_x, gx = [], []
    for e, step in enumerate(steps):
        acc = lax.dynamic_index_in_dim(paired[e], (z + zs - step) % zs, 0, keepdims=False)
        acc_x.append(acc)
        gx.append(lax.ppermute(acc, "sens", ring_perm(step)))
    for k in range(1, zs - 1):
        for e, step in enumerate(steps):
            part, g = ordered(bands[2 * e], ((z + 4 * zs - step * (k + 2)) % zs) * quarter, quarter, g)
            acc_z[e] = got_z[e] + part
            if k < zs - 2:
                got_z[e] = lax.ppermute(acc_z[e], "sens", ring_perm(step))
    for k in range(zs - 1):
        for e, step in enumerate(steps):
            c = (z + 4 * zs - step * (k + 2)) % zs
            acc_x[e] = gx[e] + lax.dynamic_index_in_dim(paired[e], c, 0, keepdims=False)
            if k < zs - 2:
                gx[e] = lax.ppermute(acc_x[e], "sens", ring_perm(step))
    outs = []
    for e in range(EV):
        theirs = lax.dynamic_slice_in_dim(acc_z[e], (1 - xh) * block, block, 0)
        kept = lax.dynamic_slice_in_dim(acc_z[e], xh * block, block, 0)
        first = kept + lax.ppermute(theirs, "sens", swap)
        outs.append(jnp.flip(jnp.concatenate([first, acc_x[e]], axis=1), axis=-1))
    return jnp.stack(outs, axis=1)


def solution(mesh):
    return jax.shard_map(
        local,
        mesh=mesh,
        in_specs=(
            P("loc", "sens", None, None),
            P("loc", None, "sens", None, None),
            P(),
            P(None, "sens"),
            P("sens", None),
        ),
        out_specs=P(("loc", "sens"), None, None),
        check_vma=False,
    )
```

```python
import jax
import jax.numpy as jnp
from jax import lax
from jax.experimental import pallas as pl
from jax.experimental.pallas import tpu as pltpu
from jax.sharding import PartitionSpec as P

NT = 256
LAGS = 512
SAMPLES = 1024
EV = 2
WIDE = LAGS + NT


def from_owners(x, axis, roots, radix=4):
    size = lax.axis_size(axis)
    me = lax.axis_index(axis)
    span = 1
    while span < size:
        radix = min(radix, size // span)
        digit = (roots // span) % radix
        mine = (me // span) % radix
        out = x
        for d in range(1, radix):
            perm = [(i, i - ((i // span) % radix) * span + (((i // span) % radix + d) % radix) * span) for i in range(size)]
            got = lax.ppermute(x, axis, perm)
            src = (mine + radix - d) % radix
            out = jnp.where((src == digit).reshape((-1,) + (1,) * (x.ndim - 1)), got, out)
        x = out
        span *= radix
    return x


def _toeplitz_kernel(chunk_ref, shift_ref, weight_ref, rev_ref, green_hbm, *refs):
    ev = chunk_ref.shape[0]
    bands, firsts, gbuf, sem = refs[:ev], refs[ev : 2 * ev], refs[2 * ev], refs[2 * ev + 1]
    rows = weight_ref.shape[0]
    count = gbuf.shape[2]
    copies = [
        pltpu.make_async_copy(
            green_hbm.at[:, pl.ds(pl.multiple_of(chunk_ref[e] * count, count), count), :],
            gbuf.at[e],
            sem.at[e],
        )
        for e in range(ev)
    ]
    for c in copies:
        c.start()

    def body(r, carry):
        for e, out_ref in enumerate(bands):
            row = rev_ref[e * rows + r]
            row = pltpu.roll(row, shift_ref[e * rows + r], 1)
            row = (row * weight_ref[r]).astype(jnp.bfloat16).astype(jnp.float32)
            row = jnp.concatenate([row[:, :LAGS], row[:, SAMPLES - NT :]], axis=1)
            wide = jnp.broadcast_to(row, (NT, WIDE))
            band = pltpu.roll(wide, 0, 1, stride=1, stride_axis=0)
            out_ref[pl.ds(pl.multiple_of(r * NT, NT), NT), :] = band[:, :LAGS].astype(out_ref.dtype)
        return carry

    lax.fori_loop(0, rows, body, 0)
    for e in range(ev):
        copies[e].wait()
        firsts[e][...] = jnp.zeros(firsts[e].shape, firsts[e].dtype)

        def mm(r, carry, e=e):
            g = gbuf[e, r]
            b = bands[e][pl.ds(pl.multiple_of(r * NT, NT), NT), :]
            firsts[e][...] += jnp.dot(g, b, preferred_element_type=jnp.float32)
            return carry

        lax.fori_loop(0, rows, mm, 0)


def toeplitz_reversed(rev, shifts, weights, green_t, chunks, count):
    rows = weights.shape[0]
    ev = rev.shape[0] // rows
    band = jax.ShapeDtypeStruct((rows * NT, LAGS), jnp.bfloat16)
    first = jax.ShapeDtypeStruct((count, LAGS), jnp.float32)
    smem = pl.BlockSpec(memory_space=pltpu.SMEM)
    vmem = pl.BlockSpec(memory_space=pltpu.VMEM)
    outs = pl.pallas_call(
        _toeplitz_kernel,
        in_specs=[smem, smem, smem, vmem, pl.BlockSpec(memory_space=pl.ANY)],
        out_specs=[vmem] * (2 * ev),
        out_shape=[band] * ev + [first] * ev,
        scratch_shapes=[
            pltpu.VMEM((ev, rows, count, NT), jnp.bfloat16),
            pltpu.SemaphoreType.DMA((ev,)),
        ],
        cost_estimate=pl.CostEstimate(
            flops=2 * ev * count * rows * NT * LAGS,
            transcendentals=0,
            bytes_accessed=ev * rows * NT * (LAGS + count) * 2,
        ),
    )(chunks, shifts, weights, rev, green_t)
    return outs[:ev], outs[ev:]


def local(green, records_buffer, owners, onsets, codes):
    point_rows = green.shape[0]
    rows = green.shape[1] * green.shape[2]
    green_t = jnp.transpose(green, (1, 2, 0, 3)).reshape(rows, point_rows, NT)
    traces = from_owners(records_buffer[0], "loc", owners).reshape(EV * rows, SAMPLES)
    i = lax.broadcasted_iota(jnp.int32, (SAMPLES, SAMPLES), 0)
    j = lax.broadcasted_iota(jnp.int32, (SAMPLES, SAMPLES), 1)
    anti = (i + j == SAMPLES - 1).astype(jnp.bfloat16)
    rev = jnp.dot(traces, anti, preferred_element_type=jnp.float32).reshape(EV * rows, 1, SAMPLES)
    shifts = ((jnp.repeat(onsets.astype(jnp.int32), 3, axis=1) - LAGS) % SAMPLES).reshape(-1)
    weights = jnp.exp2(-codes.astype(jnp.float32)).reshape(-1)

    size = lax.axis_size("sens")
    me = lax.axis_index("sens")
    xs = 2
    zs = size // xs
    z, xh = me // xs, me % xs
    quarter = point_rows // zs
    block = quarter // xs

    def piece(band, c, src=None):
        g = lax.dynamic_slice_in_dim(green_t if src is None else src, c * quarter, quarter, 1)
        return jnp.einsum("rpt,rtn->pn", g, band.reshape(rows, NT, LAGS), preferred_element_type=jnp.float32)

    def ring_perm(step):
        return [(i, ((i // xs + step) % zs) * xs + i % xs) for i in range(size)]

    steps = (1, zs - 1)
    chunks = jnp.stack([(z + zs - st) % zs for st in steps]).astype(jnp.int32)
    bands, firsts = toeplitz_reversed(rev, shifts, weights, green_t, chunks, quarter)
    g = green_t

    def ordered(e, c, g):
        return lax.optimization_barrier((piece(bands[e], c, g), green_t))

    accs = list(firsts)
    gots = [lax.ppermute(accs[e], "sens", ring_perm(step)) for e, step in enumerate(steps)]
    for k in range(zs - 1):
        for e, step in enumerate(steps):
            part, g = ordered(e, (z + 4 * zs - step * (k + 2)) % zs, g)
            accs[e] = gots[e] + part
            if k < zs - 2:
                gots[e] = lax.ppermute(accs[e], "sens", ring_perm(step))
    outs = []
    for e in range(EV):
        theirs = lax.dynamic_slice_in_dim(accs[e], (1 - xh) * block, block, 0)
        kept = lax.dynamic_slice_in_dim(accs[e], xh * block, block, 0)
        got = lax.ppermute(theirs, "sens", [(i, i ^ 1) for i in range(size)])
        outs.append(jnp.flip(kept, axis=-1) + jnp.flip(got, axis=-1))
    return jnp.stack(outs, axis=1)


def solution(mesh):
    return jax.shard_map(
        local,
        mesh=mesh,
        in_specs=(
            P("loc", "sens", None, None),
            P("loc", None, "sens", None, None),
            P(),
            P(None, "sens"),
            P("sens", None),
        ),
        out_specs=P(("loc", "sens"), None, None),
        check_vma=False,
    )
```

```python
import jax
import jax.numpy as jnp
from jax import lax
from jax.experimental import pallas as pl
from jax.experimental.pallas import tpu as pltpu
from jax.sharding import PartitionSpec as P

NT = 256
LAGS = 512
SAMPLES = 1024
EV = 2
WIDE = LAGS + NT


def from_owners(x, axis, roots, radix=4):
    size = lax.axis_size(axis)
    me = lax.axis_index(axis)
    span = 1
    while span < size:
        radix = min(radix, size // span)
        digit = (roots // span) % radix
        mine = (me // span) % radix
        out = x
        for d in range(1, radix):
            perm = [(i, i - ((i // span) % radix) * span + (((i // span) % radix + d) % radix) * span) for i in range(size)]
            got = lax.ppermute(x, axis, perm)
            src = (mine + radix - d) % radix
            out = jnp.where((src == digit).reshape((-1,) + (1,) * (x.ndim - 1)), got, out)
        x = out
        span *= radix
    return x


def _toeplitz_kernel(shift_ref, weight_ref, rev_ref, *out_refs):
    rows = weight_ref.shape[0]

    def body(r, carry):
        for e, out_ref in enumerate(out_refs):
            row = rev_ref[e * rows + r]
            row = pltpu.roll(row, shift_ref[e * rows + r], 1)
            row = (row * weight_ref[r]).astype(jnp.bfloat16).astype(jnp.float32)
            row = jnp.concatenate([row[:, :LAGS], row[:, SAMPLES - NT :]], axis=1)
            wide = jnp.broadcast_to(row, (NT, WIDE))
            band = pltpu.roll(wide, 0, 1, stride=1, stride_axis=0)
            out_ref[pl.ds(pl.multiple_of(r * NT, NT), NT), :] = band[:, :LAGS].astype(out_ref.dtype)
        return carry

    lax.fori_loop(0, rows, body, 0)


def toeplitz_reversed(rev, shifts, weights):
    rows = weights.shape[0]
    ev = rev.shape[0] // rows
    band = jax.ShapeDtypeStruct((rows * NT, LAGS), jnp.bfloat16)
    return pl.pallas_call(
        _toeplitz_kernel,
        in_specs=[
            pl.BlockSpec(memory_space=pltpu.SMEM),
            pl.BlockSpec(memory_space=pltpu.SMEM),
            pl.BlockSpec(memory_space=pltpu.VMEM),
        ],
        out_specs=[pl.BlockSpec(memory_space=pltpu.VMEM)] * ev,
        out_shape=[band] * ev,
        cost_estimate=pl.CostEstimate(flops=0, transcendentals=0, bytes_accessed=ev * rows * NT * LAGS * 2),
        compiler_params=pltpu.CompilerParams(vmem_limit_bytes=24 * 1024 * 1024),
    )(shifts, weights, rev)


def local(green, records_buffer, owners, onsets, codes):
    point_rows = green.shape[0]
    rows = green.shape[1] * green.shape[2]
    green_t = jnp.transpose(green, (1, 2, 0, 3)).reshape(rows, point_rows, NT)
    traces = from_owners(records_buffer[0], "loc", owners).reshape(EV * rows, SAMPLES)
    i = lax.broadcasted_iota(jnp.int32, (SAMPLES, SAMPLES), 0)
    j = lax.broadcasted_iota(jnp.int32, (SAMPLES, SAMPLES), 1)
    anti = (i + j == SAMPLES - 1).astype(jnp.bfloat16)
    rev = jnp.dot(traces, anti, preferred_element_type=jnp.float32).reshape(EV * rows, 1, SAMPLES)
    shifts = ((jnp.repeat(onsets.astype(jnp.int32), 3, axis=1) - LAGS) % SAMPLES).reshape(-1)
    weights = jnp.exp2(-codes.astype(jnp.float32)).reshape(-1)
    bands = toeplitz_reversed(rev, shifts, weights)

    size = lax.axis_size("sens")
    me = lax.axis_index("sens")
    xs = 2
    zs = size // xs
    z, xh = me // xs, me % xs
    quarter = point_rows // zs
    block = quarter // xs

    def piece(band, c, src=None):
        g = lax.dynamic_slice_in_dim(green_t if src is None else src, c * quarter, quarter, 1)
        return jnp.einsum("rpt,rtn->pn", g, band.reshape(rows, NT, LAGS), preferred_element_type=jnp.float32)

    def ring_perm(step):
        return [(i, ((i // xs + step) % zs) * xs + i % xs) for i in range(size)]

    steps = (1, zs - 1)
    g = green_t

    def ordered(e, c, g):
        return lax.optimization_barrier((piece(bands[e], c, g), green_t))

    accs, gots = [], []
    for e, step in enumerate(steps):
        acc, g = ordered(e, (z + zs - step) % zs, g)
        accs.append(acc)
        gots.append(lax.ppermute(acc, "sens", ring_perm(step)))
    for k in range(zs - 1):
        for e, step in enumerate(steps):
            part, g = ordered(e, (z + 4 * zs - step * (k + 2)) % zs, g)
            accs[e] = gots[e] + part
            if k < zs - 2:
                gots[e] = lax.ppermute(accs[e], "sens", ring_perm(step))
    outs = []
    for e in range(EV):
        theirs = lax.dynamic_slice_in_dim(accs[e], (1 - xh) * block, block, 0)
        kept = lax.dynamic_slice_in_dim(accs[e], xh * block, block, 0)
        got = lax.ppermute(theirs, "sens", [(i, i ^ 1) for i in range(size)])
        outs.append(jnp.flip(kept, axis=-1) + jnp.flip(got, axis=-1))
    return jnp.stack(outs, axis=1)


def solution(mesh):
    return jax.shard_map(
        local,
        mesh=mesh,
        in_specs=(
            P("loc", "sens", None, None),
            P("loc", None, "sens", None, None),
            P(),
            P(None, "sens"),
            P("sens", None),
        ),
        out_specs=P(("loc", "sens"), None, None),
        check_vma=False,
    )
```

```python
import jax
import jax.numpy as jnp
from jax import lax
from jax.experimental import pallas as pl
from jax.experimental.pallas import tpu as pltpu
from jax.sharding import PartitionSpec as P

NT = 256
LAGS = 512
SAMPLES = 1024
EV = 2
WIDE = LAGS + NT


def from_owners(x, axis, roots, radix=4):
    size = lax.axis_size(axis)
    me = lax.axis_index(axis)
    span = 1
    while span < size:
        radix = min(radix, size // span)
        digit = (roots // span) % radix
        mine = (me // span) % radix
        out = x
        for d in range(1, radix):
            perm = [(i, i - ((i // span) % radix) * span + (((i // span) % radix + d) % radix) * span) for i in range(size)]
            got = lax.ppermute(x, axis, perm)
            src = (mine + radix - d) % radix
            out = jnp.where((src == digit).reshape((-1,) + (1,) * (x.ndim - 1)), got, out)
        x = out
        span *= radix
    return x


def _toeplitz_kernel(shift_ref, weight_ref, rev_ref, *out_refs):
    rows = weight_ref.shape[0]

    def body(r, carry):
        for e, out_ref in enumerate(out_refs):
            row = rev_ref[e * rows + r]
            row = pltpu.roll(row, shift_ref[e * rows + r], 1)
            row = (row * weight_ref[r]).astype(jnp.bfloat16).astype(jnp.float32)
            row = jnp.concatenate([row[:, :LAGS], row[:, SAMPLES - NT :]], axis=1)
            wide = jnp.broadcast_to(row, (NT, WIDE))
            band = pltpu.roll(wide, 0, 1, stride=1, stride_axis=0)
            out_ref[pl.ds(pl.multiple_of(r * NT, NT), NT), :] = band[:, :LAGS].astype(out_ref.dtype)
        return carry

    lax.fori_loop(0, rows, body, 0)


def toeplitz_reversed(rev, shifts, weights):
    rows = weights.shape[0]
    ev = rev.shape[0] // rows
    band = jax.ShapeDtypeStruct((rows * NT, LAGS), jnp.bfloat16)
    return pl.pallas_call(
        _toeplitz_kernel,
        in_specs=[
            pl.BlockSpec(memory_space=pltpu.SMEM),
            pl.BlockSpec(memory_space=pltpu.SMEM),
            pl.BlockSpec(memory_space=pltpu.VMEM),
        ],
        out_specs=[pl.BlockSpec(memory_space=pltpu.VMEM)] * ev,
        out_shape=[band] * ev,
        cost_estimate=pl.CostEstimate(flops=0, transcendentals=0, bytes_accessed=ev * rows * NT * LAGS * 2),
        compiler_params=pltpu.CompilerParams(vmem_limit_bytes=24 * 1024 * 1024),
    )(shifts, weights, rev)


def local(green, records_buffer, owners, onsets, codes):
    point_rows = green.shape[0]
    rows = green.shape[1] * green.shape[2]
    green_t = jnp.transpose(green, (1, 2, 0, 3)).reshape(rows, point_rows, NT)
    traces = from_owners(records_buffer[0], "loc", owners).reshape(EV * rows, SAMPLES)
    i = lax.broadcasted_iota(jnp.int32, (SAMPLES, SAMPLES), 0)
    j = lax.broadcasted_iota(jnp.int32, (SAMPLES, SAMPLES), 1)
    anti = (i + j == SAMPLES - 1).astype(jnp.bfloat16)
    rev = jnp.dot(traces, anti, preferred_element_type=jnp.float32).reshape(EV * rows, 1, SAMPLES)
    shifts = ((jnp.repeat(onsets.astype(jnp.int32), 3, axis=1) - LAGS) % SAMPLES).reshape(-1)
    weights = jnp.exp2(-codes.astype(jnp.float32)).reshape(-1)
    bands = [
        toeplitz_reversed(rev[e * rows : (e + 1) * rows], shifts[e * rows : (e + 1) * rows], weights)[0]
        for e in range(EV)
    ]

    size = lax.axis_size("sens")
    me = lax.axis_index("sens")
    xs = 2
    zs = size // xs
    z, xh = me // xs, me % xs
    quarter = point_rows // zs
    block = quarter // xs

    def piece(band, c, src=None):
        g = lax.dynamic_slice_in_dim(green_t if src is None else src, c * quarter, quarter, 1)
        return jnp.einsum("rpt,rtn->pn", g, band.reshape(rows, NT, LAGS), preferred_element_type=jnp.float32)

    def ring_perm(step):
        return [(i, ((i // xs + step) % zs) * xs + i % xs) for i in range(size)]

    steps = (1, zs - 1)
    g = green_t

    def ordered(e, c, g):
        return lax.optimization_barrier((piece(bands[e], c, g), green_t))

    accs, gots = [], []
    for e, step in enumerate(steps):
        acc, g = ordered(e, (z + zs - step) % zs, g)
        accs.append(acc)
        gots.append(lax.ppermute(acc, "sens", ring_perm(step)))
    for k in range(zs - 1):
        for e, step in enumerate(steps):
            part, g = ordered(e, (z + 4 * zs - step * (k + 2)) % zs, g)
            accs[e] = gots[e] + part
            if k < zs - 2:
                gots[e] = lax.ppermute(accs[e], "sens", ring_perm(step))
    outs = []
    for e in range(EV):
        theirs = lax.dynamic_slice_in_dim(accs[e], (1 - xh) * block, block, 0)
        kept = lax.dynamic_slice_in_dim(accs[e], xh * block, block, 0)
        got = lax.ppermute(theirs, "sens", [(i, i ^ 1) for i in range(size)])
        outs.append(jnp.flip(kept, axis=-1) + jnp.flip(got, axis=-1))
    return jnp.stack(outs, axis=1)


def solution(mesh):
    return jax.shard_map(
        local,
        mesh=mesh,
        in_specs=(
            P("loc", "sens", None, None),
            P("loc", None, "sens", None, None),
            P(),
            P(None, "sens"),
            P("sens", None),
        ),
        out_specs=P(("loc", "sens"), None, None),
        check_vma=False,
    )
```

```python
import jax
import jax.numpy as jnp
from jax import lax
from jax.experimental import pallas as pl
from jax.experimental.pallas import tpu as pltpu
from jax.sharding import PartitionSpec as P

NT = 256
LAGS = 512
SAMPLES = 1024
EV = 2
WIDE = LAGS + NT


def from_owners(x, axis, roots, radix=4):
    size = lax.axis_size(axis)
    me = lax.axis_index(axis)
    spans, span = [], 1
    while span < size:
        spans.append((span, min(radix, size // span)))
        span *= radix
    for span, r in reversed(spans):
        digit = (roots // span) % r
        mine = (me // span) % r
        out = x
        for d in range(1, r):
            perm = [(i, i - ((i // span) % r) * span + (((i // span) % r + d) % r) * span) for i in range(size)]
            got = lax.ppermute(x, axis, perm)
            src = (mine + r - d) % r
            out = jnp.where((src == digit).reshape((-1,) + (1,) * (x.ndim - 1)), got, out)
        x = out
    return x


def _toeplitz_kernel(shift_ref, weight_ref, rev_ref, *out_refs):
    rows = weight_ref.shape[0]

    def body(r, carry):
        for e, out_ref in enumerate(out_refs):
            row = rev_ref[e * rows + r]
            row = pltpu.roll(row, shift_ref[e * rows + r], 1)
            row = (row * weight_ref[r]).astype(jnp.bfloat16).astype(jnp.float32)
            row = jnp.concatenate([row[:, :LAGS], row[:, SAMPLES - NT :]], axis=1)
            wide = jnp.broadcast_to(row, (NT, WIDE))
            band = pltpu.roll(wide, 0, 1, stride=1, stride_axis=0)
            out_ref[pl.ds(pl.multiple_of(r * NT, NT), NT), :] = band[:, :LAGS].astype(out_ref.dtype)
        return carry

    lax.fori_loop(0, rows, body, 0)


def toeplitz_reversed(rev, shifts, weights):
    rows = weights.shape[0]
    ev = rev.shape[0] // rows
    band = jax.ShapeDtypeStruct((rows * NT, LAGS), jnp.bfloat16)
    return pl.pallas_call(
        _toeplitz_kernel,
        in_specs=[
            pl.BlockSpec(memory_space=pltpu.SMEM),
            pl.BlockSpec(memory_space=pltpu.SMEM),
            pl.BlockSpec(memory_space=pltpu.VMEM),
        ],
        out_specs=[pl.BlockSpec(memory_space=pltpu.VMEM)] * ev,
        out_shape=[band] * ev,
        cost_estimate=pl.CostEstimate(flops=0, transcendentals=0, bytes_accessed=ev * rows * NT * LAGS * 2),
        compiler_params=pltpu.CompilerParams(vmem_limit_bytes=24 * 1024 * 1024),
    )(shifts, weights, rev)


def local(green, records_buffer, owners, onsets, codes):
    point_rows = green.shape[0]
    rows = green.shape[1] * green.shape[2]
    green_t = jnp.transpose(green, (1, 2, 0, 3)).reshape(rows, point_rows, NT)
    traces = from_owners(records_buffer[0], "loc", owners).reshape(EV * rows, SAMPLES)
    i = lax.broadcasted_iota(jnp.int32, (SAMPLES, SAMPLES), 0)
    j = lax.broadcasted_iota(jnp.int32, (SAMPLES, SAMPLES), 1)
    anti = (i + j == SAMPLES - 1).astype(jnp.bfloat16)
    rev = jnp.dot(traces, anti, preferred_element_type=jnp.float32).reshape(EV * rows, 1, SAMPLES)
    shifts = ((jnp.repeat(onsets.astype(jnp.int32), 3, axis=1) - LAGS) % SAMPLES).reshape(-1)
    weights = jnp.exp2(-codes.astype(jnp.float32)).reshape(-1)
    bands = toeplitz_reversed(rev, shifts, weights)

    size = lax.axis_size("sens")
    me = lax.axis_index("sens")
    xs = 2
    zs = size // xs
    z, xh = me // xs, me % xs
    quarter = point_rows // zs
    block = quarter // xs

    def piece(band, c, src=None):
        g = lax.dynamic_slice_in_dim(green_t if src is None else src, c * quarter, quarter, 1)
        return jnp.einsum("rpt,rtn->pn", g, band.reshape(rows, NT, LAGS), preferred_element_type=jnp.float32)

    def ring_perm(step):
        return [(i, ((i // xs + step) % zs) * xs + i % xs) for i in range(size)]

    steps = (1, zs - 1)
    g = green_t

    def ordered(e, c, g):
        return lax.optimization_barrier((piece(bands[e], c, g), green_t))

    accs, gots = [], []
    for e, step in enumerate(steps):
        acc, g = ordered(e, (z + zs - step) % zs, g)
        accs.append(acc)
        gots.append(lax.ppermute(acc, "sens", ring_perm(step)))
    for k in range(zs - 1):
        for e, step in enumerate(steps):
            part, g = ordered(e, (z + 4 * zs - step * (k + 2)) % zs, g)
            accs[e] = gots[e] + part
            if k < zs - 2:
                gots[e] = lax.ppermute(accs[e], "sens", ring_perm(step))
    outs = []
    for e in range(EV):
        theirs = lax.dynamic_slice_in_dim(accs[e], (1 - xh) * block, block, 0)
        kept = lax.dynamic_slice_in_dim(accs[e], xh * block, block, 0)
        got = lax.ppermute(theirs, "sens", [(i, i ^ 1) for i in range(size)])
        outs.append(jnp.flip(kept, axis=-1) + jnp.flip(got, axis=-1))
    return jnp.stack(outs, axis=1)


def solution(mesh):
    return jax.shard_map(
        local,
        mesh=mesh,
        in_specs=(
            P("loc", "sens", None, None),
            P("loc", None, "sens", None, None),
            P(),
            P(None, "sens"),
            P("sens", None),
        ),
        out_specs=P(("loc", "sens"), None, None),
        check_vma=False,
    )
```

```python
import jax
import jax.numpy as jnp
from jax import lax
from jax.experimental import pallas as pl
from jax.experimental.pallas import tpu as pltpu
from jax.sharding import PartitionSpec as P

NT = 256
LAGS = 512
SAMPLES = 1024
EV = 2
WIDE = LAGS + NT


def from_owners(x, axis, roots, radix=4):
    size = lax.axis_size(axis)
    me = lax.axis_index(axis)
    span = 1
    while span < size:
        radix = min(radix, size // span)
        digit = (roots // span) % radix
        mine = (me // span) % radix
        out = x
        for d in range(1, radix):
            perm = [(i, i - ((i // span) % radix) * span + (((i // span) % radix + d) % radix) * span) for i in range(size)]
            got = lax.ppermute(x, axis, perm)
            src = (mine + radix - d) % radix
            out = jnp.where((src == digit).reshape((-1,) + (1,) * (x.ndim - 1)), got, out)
        x = out
        span *= radix
    return x


def _toeplitz_kernel(shift_ref, weight_ref, rev_ref, *out_refs):
    rows = weight_ref.shape[0]

    def body(r, carry):
        for e, out_ref in enumerate(out_refs):
            row = rev_ref[r * len(out_refs) + e]
            row = pltpu.roll(row, shift_ref[e * rows + r], 1)
            row = (row * weight_ref[r]).astype(jnp.bfloat16).astype(jnp.float32)
            row = jnp.concatenate([row[:, :LAGS], row[:, SAMPLES - NT :]], axis=1)
            wide = jnp.broadcast_to(row, (NT, WIDE))
            band = pltpu.roll(wide, 0, 1, stride=1, stride_axis=0)
            out_ref[pl.ds(pl.multiple_of(r * NT, NT), NT), :] = band[:, :LAGS].astype(out_ref.dtype)
        return carry

    lax.fori_loop(0, rows, body, 0)


def toeplitz_reversed(rev, shifts, weights):
    rows = weights.shape[0]
    ev = rev.shape[0] // rows
    band = jax.ShapeDtypeStruct((rows * NT, LAGS), jnp.bfloat16)
    return pl.pallas_call(
        _toeplitz_kernel,
        in_specs=[
            pl.BlockSpec(memory_space=pltpu.SMEM),
            pl.BlockSpec(memory_space=pltpu.SMEM),
            pl.BlockSpec(memory_space=pltpu.VMEM),
        ],
        out_specs=[pl.BlockSpec(memory_space=pltpu.VMEM)] * ev,
        out_shape=[band] * ev,
        cost_estimate=pl.CostEstimate(flops=0, transcendentals=0, bytes_accessed=ev * rows * NT * LAGS * 2),
        compiler_params=pltpu.CompilerParams(vmem_limit_bytes=24 * 1024 * 1024),
    )(shifts, weights, rev)


def local(green, records_buffer, owners, onsets, codes):
    point_rows = green.shape[0]
    rows = green.shape[1] * green.shape[2]
    green_t = jnp.transpose(green, (1, 2, 0, 3)).reshape(rows, point_rows, NT)
    records = jnp.transpose(records_buffer[0], (1, 2, 0, 3)).reshape(rows * EV, SAMPLES)
    traces = from_owners(records, "loc", jnp.tile(owners, rows))
    i = lax.broadcasted_iota(jnp.int32, (SAMPLES, SAMPLES), 0)
    j = lax.broadcasted_iota(jnp.int32, (SAMPLES, SAMPLES), 1)
    anti = (i + j == SAMPLES - 1).astype(jnp.bfloat16)
    rev = jnp.dot(traces, anti, preferred_element_type=jnp.float32).reshape(EV * rows, 1, SAMPLES)
    shifts = ((jnp.repeat(onsets.astype(jnp.int32), 3, axis=1) - LAGS) % SAMPLES).reshape(-1)
    weights = jnp.exp2(-codes.astype(jnp.float32)).reshape(-1)
    bands = toeplitz_reversed(rev, shifts, weights)

    size = lax.axis_size("sens")
    me = lax.axis_index("sens")
    xs = 2
    zs = size // xs
    z, xh = me // xs, me % xs
    quarter = point_rows // zs
    block = quarter // xs

    def piece(band, c, src=None):
        g = lax.dynamic_slice_in_dim(green_t if src is None else src, c * quarter, quarter, 1)
        return jnp.einsum("rpt,rtn->pn", g, band.reshape(rows, NT, LAGS), preferred_element_type=jnp.float32)

    def ring_perm(step):
        return [(i, ((i // xs + step) % zs) * xs + i % xs) for i in range(size)]

    steps = (1, zs - 1)
    g = green_t

    def ordered(e, c, g):
        return lax.optimization_barrier((piece(bands[e], c, g), green_t))

    accs, gots = [], []
    for e, step in enumerate(steps):
        acc, g = ordered(e, (z + zs - step) % zs, g)
        accs.append(acc)
        gots.append(lax.ppermute(acc, "sens", ring_perm(step)))
    for k in range(zs - 1):
        for e, step in enumerate(steps):
            part, g = ordered(e, (z + 4 * zs - step * (k + 2)) % zs, g)
            accs[e] = gots[e] + part
            if k < zs - 2:
                gots[e] = lax.ppermute(accs[e], "sens", ring_perm(step))
    outs = []
    for e in range(EV):
        theirs = lax.dynamic_slice_in_dim(accs[e], (1 - xh) * block, block, 0)
        kept = lax.dynamic_slice_in_dim(accs[e], xh * block, block, 0)
        got = lax.ppermute(theirs, "sens", [(i, i ^ 1) for i in range(size)])
        outs.append(jnp.flip(kept, axis=-1) + jnp.flip(got, axis=-1))
    return jnp.stack(outs, axis=1)


def solution(mesh):
    return jax.shard_map(
        local,
        mesh=mesh,
        in_specs=(
            P("loc", "sens", None, None),
            P("loc", None, "sens", None, None),
            P(),
            P(None, "sens"),
            P("sens", None),
        ),
        out_specs=P(("loc", "sens"), None, None),
        check_vma=False,
    )
```

```python
import jax
import jax.numpy as jnp
from jax import lax
from jax.experimental import pallas as pl
from jax.experimental.pallas import tpu as pltpu
from jax.sharding import PartitionSpec as P

NT = 256
LAGS = 512
SAMPLES = 1024
EV = 2
WIDE = LAGS + NT


def from_owners(x, axis, roots, radix=4):
    size = lax.axis_size(axis)
    me = lax.axis_index(axis)
    span = 1
    while span < size:
        radix = min(radix, size // span)
        digit = (roots // span) % radix
        mine = (me // span) % radix
        out = x
        for d in range(1, radix):
            perm = [(i, i - ((i // span) % radix) * span + (((i // span) % radix + d) % radix) * span) for i in range(size)]
            got = lax.ppermute(x, axis, perm)
            src = (mine + radix - d) % radix
            out = jnp.where((src == digit).reshape((-1,) + (1,) * (x.ndim - 1)), got, out)
        x = out
        span *= radix
    return x


def _toeplitz_kernel(shift_ref, weight_ref, rev_ref, *out_refs):
    rows = weight_ref.shape[0]

    def body(r, carry):
        for e, out_ref in enumerate(out_refs):
            row = rev_ref[e * rows + r]
            row = pltpu.roll(row, shift_ref[e * rows + r], 1)
            row = (row * weight_ref[r]).astype(jnp.bfloat16)
            row = jnp.concatenate([row[:, :LAGS], row[:, SAMPLES - NT :]], axis=1)
            wide = jnp.broadcast_to(row, (NT, WIDE))
            band = pltpu.roll(wide, 0, 1, stride=1, stride_axis=0)
            out_ref[pl.ds(pl.multiple_of(r * NT, NT), NT), :] = band[:, :LAGS].astype(out_ref.dtype)
        return carry

    lax.fori_loop(0, rows, body, 0)


def toeplitz_reversed(rev, shifts, weights):
    rows = weights.shape[0]
    ev = rev.shape[0] // rows
    band = jax.ShapeDtypeStruct((rows * NT, LAGS), jnp.bfloat16)
    return pl.pallas_call(
        _toeplitz_kernel,
        in_specs=[
            pl.BlockSpec(memory_space=pltpu.SMEM),
            pl.BlockSpec(memory_space=pltpu.SMEM),
            pl.BlockSpec(memory_space=pltpu.VMEM),
        ],
        out_specs=[pl.BlockSpec(memory_space=pltpu.VMEM)] * ev,
        out_shape=[band] * ev,
        cost_estimate=pl.CostEstimate(flops=0, transcendentals=0, bytes_accessed=ev * rows * NT * LAGS * 2),
        compiler_params=pltpu.CompilerParams(vmem_limit_bytes=24 * 1024 * 1024),
    )(shifts, weights, rev)


def local(green, records_buffer, owners, onsets, codes):
    point_rows = green.shape[0]
    rows = green.shape[1] * green.shape[2]
    green_t = jnp.transpose(green, (1, 2, 0, 3)).reshape(rows, point_rows, NT)
    traces = from_owners(records_buffer[0], "loc", owners).reshape(EV * rows, SAMPLES)
    i = lax.broadcasted_iota(jnp.int32, (SAMPLES, SAMPLES), 0)
    j = lax.broadcasted_iota(jnp.int32, (SAMPLES, SAMPLES), 1)
    anti = (i + j == SAMPLES - 1).astype(jnp.bfloat16)
    rev = jnp.dot(traces, anti, preferred_element_type=jnp.float32).reshape(EV * rows, 1, SAMPLES)
    shifts = ((jnp.repeat(onsets.astype(jnp.int32), 3, axis=1) - LAGS) % SAMPLES).reshape(-1)
    weights = jnp.exp2(-codes.astype(jnp.float32)).reshape(-1)
    bands = toeplitz_reversed(rev, shifts, weights)

    size = lax.axis_size("sens")
    me = lax.axis_index("sens")
    xs = 2
    zs = size // xs
    z, xh = me // xs, me % xs
    quarter = point_rows // zs
    block = quarter // xs

    def piece(band, c, src=None):
        g = lax.dynamic_slice_in_dim(green_t if src is None else src, c * quarter, quarter, 1)
        return jnp.einsum("rpt,rtn->pn", g, band.reshape(rows, NT, LAGS), preferred_element_type=jnp.float32)

    def ring_perm(step):
        return [(i, ((i // xs + step) % zs) * xs + i % xs) for i in range(size)]

    steps = (1, zs - 1)
    g = green_t

    def ordered(e, c, g):
        return lax.optimization_barrier((piece(bands[e], c, g), green_t))

    accs, gots = [], []
    for e, step in enumerate(steps):
        acc, g = ordered(e, (z + zs - step) % zs, g)
        accs.append(acc)
        gots.append(lax.ppermute(acc, "sens", ring_perm(step)))
    for k in range(zs - 1):
        for e, step in enumerate(steps):
            part, g = ordered(e, (z + 4 * zs - step * (k + 2)) % zs, g)
            accs[e] = gots[e] + part
            if k < zs - 2:
                gots[e] = lax.ppermute(accs[e], "sens", ring_perm(step))
    outs = []
    for e in range(EV):
        theirs = lax.dynamic_slice_in_dim(accs[e], (1 - xh) * block, block, 0)
        kept = lax.dynamic_slice_in_dim(accs[e], xh * block, block, 0)
        got = lax.ppermute(theirs, "sens", [(i, i ^ 1) for i in range(size)])
        outs.append(jnp.flip(kept, axis=-1) + jnp.flip(got, axis=-1))
    return jnp.stack(outs, axis=1)


def solution(mesh):
    return jax.shard_map(
        local,
        mesh=mesh,
        in_specs=(
            P("loc", "sens", None, None),
            P("loc", None, "sens", None, None),
            P(),
            P(None, "sens"),
            P("sens", None),
        ),
        out_specs=P(("loc", "sens"), None, None),
        check_vma=False,
    )
```

```python
import jax
import jax.numpy as jnp
from jax import lax
from jax.experimental import pallas as pl
from jax.experimental.pallas import tpu as pltpu
from jax.sharding import PartitionSpec as P

NT = 256
LAGS = 512
SAMPLES = 1024
EV = 2
WIDE = LAGS + NT


def from_owners(x, axis, roots, radix=4):
    size = lax.axis_size(axis)
    me = lax.axis_index(axis)
    span = 1
    while span < size:
        radix = min(radix, size // span)
        digit = (roots // span) % radix
        mine = (me // span) % radix
        out = x
        for d in range(1, radix):
            perm = [(i, i - ((i // span) % radix) * span + (((i // span) % radix + d) % radix) * span) for i in range(size)]
            got = lax.ppermute(x, axis, perm)
            src = (mine + radix - d) % radix
            out = jnp.where((src == digit).reshape((-1,) + (1,) * (x.ndim - 1)), got, out)
        x = out
        span *= radix
    return x


def _toeplitz_kernel(shift_ref, weight_ref, rev_ref, *out_refs):
    rows = weight_ref.shape[0]

    def body(r, carry):
        for e, out_ref in enumerate(out_refs):
            row = rev_ref[e * rows + r]
            row = pltpu.roll(row, shift_ref[e * rows + r], 1)
            row = (row * weight_ref[r]).astype(jnp.bfloat16).astype(jnp.float32)
            row = jnp.concatenate([row[:, :LAGS], row[:, SAMPLES - NT :]], axis=1)
            wide = jnp.broadcast_to(row, (NT, WIDE))
            band = pltpu.roll(wide, 0, 1, stride=1, stride_axis=0)
            out_ref[pl.ds(pl.multiple_of(r * NT, NT), NT), :] = band[:, :LAGS].astype(out_ref.dtype)
        return carry

    lax.fori_loop(0, rows, body, 0, unroll=3)


def toeplitz_reversed(rev, shifts, weights):
    rows = weights.shape[0]
    ev = rev.shape[0] // rows
    band = jax.ShapeDtypeStruct((rows * NT, LAGS), jnp.bfloat16)
    return pl.pallas_call(
        _toeplitz_kernel,
        in_specs=[
            pl.BlockSpec(memory_space=pltpu.SMEM),
            pl.BlockSpec(memory_space=pltpu.SMEM),
            pl.BlockSpec(memory_space=pltpu.VMEM),
        ],
        out_specs=[pl.BlockSpec(memory_space=pltpu.VMEM)] * ev,
        out_shape=[band] * ev,
        cost_estimate=pl.CostEstimate(flops=0, transcendentals=0, bytes_accessed=ev * rows * NT * LAGS * 2),
        compiler_params=pltpu.CompilerParams(vmem_limit_bytes=24 * 1024 * 1024),
    )(shifts, weights, rev)


def local(green, records_buffer, owners, onsets, codes):
    point_rows = green.shape[0]
    rows = green.shape[1] * green.shape[2]
    green_t = jnp.transpose(green, (1, 2, 0, 3)).reshape(rows, point_rows, NT)
    traces = from_owners(records_buffer[0], "loc", owners).reshape(EV * rows, SAMPLES)
    i = lax.broadcasted_iota(jnp.int32, (SAMPLES, SAMPLES), 0)
    j = lax.broadcasted_iota(jnp.int32, (SAMPLES, SAMPLES), 1)
    anti = (i + j == SAMPLES - 1).astype(jnp.bfloat16)
    rev = jnp.dot(traces, anti, preferred_element_type=jnp.float32).reshape(EV * rows, 1, SAMPLES)
    shifts = ((jnp.repeat(onsets.astype(jnp.int32), 3, axis=1) - LAGS) % SAMPLES).reshape(-1)
    weights = jnp.exp2(-codes.astype(jnp.float32)).reshape(-1)
    bands = toeplitz_reversed(rev, shifts, weights)

    size = lax.axis_size("sens")
    me = lax.axis_index("sens")
    xs = 2
    zs = size // xs
    z, xh = me // xs, me % xs
    quarter = point_rows // zs
    block = quarter // xs

    def piece(band, c, src=None):
        g = lax.dynamic_slice_in_dim(green_t if src is None else src, c * quarter, quarter, 1)
        return jnp.einsum("rpt,rtn->pn", g, band.reshape(rows, NT, LAGS), preferred_element_type=jnp.float32)

    def ring_perm(step):
        return [(i, ((i // xs + step) % zs) * xs + i % xs) for i in range(size)]

    steps = (1, zs - 1)
    g = green_t

    def ordered(e, c, g):
        return lax.optimization_barrier((piece(bands[e], c, g), green_t))

    accs, gots = [], []
    for e, step in enumerate(steps):
        acc, g = ordered(e, (z + zs - step) % zs, g)
        accs.append(acc)
        gots.append(lax.ppermute(acc, "sens", ring_perm(step)))
    for k in range(zs - 1):
        for e, step in enumerate(steps):
            part, g = ordered(e, (z + 4 * zs - step * (k + 2)) % zs, g)
            accs[e] = gots[e] + part
            if k < zs - 2:
                gots[e] = lax.ppermute(accs[e], "sens", ring_perm(step))
    outs = []
    for e in range(EV):
        theirs = lax.dynamic_slice_in_dim(accs[e], (1 - xh) * block, block, 0)
        kept = lax.dynamic_slice_in_dim(accs[e], xh * block, block, 0)
        got = lax.ppermute(theirs, "sens", [(i, i ^ 1) for i in range(size)])
        outs.append(jnp.flip(kept, axis=-1) + jnp.flip(got, axis=-1))
    return jnp.stack(outs, axis=1)


def solution(mesh):
    return jax.shard_map(
        local,
        mesh=mesh,
        in_specs=(
            P("loc", "sens", None, None),
            P("loc", None, "sens", None, None),
            P(),
            P(None, "sens"),
            P("sens", None),
        ),
        out_specs=P(("loc", "sens"), None, None),
        check_vma=False,
    )
```
